128 devices in a mesh: space: 64 (over y, z_hi, x, core), vec: 2 (over z_lo).
Axes of the slice: x: 4, y: 4, z: 4 (z_hi: 2, z_lo: 2; z = z_hi * 2 + z_lo), core: 2. Of those that a mesh axis runs over, the one named last changes fastest.
Arguments:
- potential: float32 [64, 128, 256], P('space'), may hold values from -8.25 to 8.25
- start_basis: float32 [16, 64, 128, 256], P('vec', 'space'), may hold values from -6 to 6
Outputs:
- new_basis: float32 [16, 64, 128, 256], P('vec', 'space')
- rayleigh: float32 [16, 16], replicated
The draws below stay inside these ranges and needn't reach their ends.
All inputs are finite; a program needn't handle non-finite values.
Results may differ from the reference program's by a relative error of at most 0.0003.
Values sent between devices are 32-bit elements; how exact they have to be, the bound alone decides.
No kernel may reach another device: no remote copies, remote signals or barrier semaphores. Data moves between devices by JAX's collectives and lax.ppermute only.
A program may use at most 64 MiB of HBM per device.

```python
import jax
import jax.numpy as jnp
from jax import lax

NB = 16
LY = 128
LX = 256
NSWEEP = 3
NZ = 64


def block_scale(stream_key, extent, cuts, smallest, top_value):
    def one(dim, parts):
        draws = jax.random.uniform(jax.random.fold_in(jax.random.fold_in(stream_key, 6), dim), (parts,), jnp.float32, smallest / len(cuts), top_value / len(cuts))
        return jnp.repeat(jnp.exp(draws), extent[dim] // parts).reshape((-1,) + (1,) * (len(extent) - dim - 1))

    gain = one(*cuts[0])
    for cut in cuts[1:]:
        gain = gain * one(*cut)
    return gain


def scatter_about(rng, extent, scale, reach, pieces=(), held_as=jnp.bfloat16):
    factor_of = block_scale(rng, extent, pieces, -0.22, 0.18) if pieces else 1.0
    array = jax.random.normal(rng, extent, jnp.float32) * scale * factor_of
    return jnp.minimum(jnp.maximum(array, -reach), reach).astype(held_as)


def setup_inputs(seed: int = 0) -> dict:
    arg_keys = jax.random.split(jax.random.key(seed), 3)
    potential = jnp.clip(jax.random.uniform(arg_keys[0], (NZ, LY, LX), jnp.float32, -8.25, 8.25) * block_scale(arg_keys[0], (NZ, LY, LX), ((0, 64),), -0.4, 0.0), -8.25, 8.25)
    start_basis = scatter_about(arg_keys[1], (NB, NZ, LY, LX), 1.0, 6.0, ((0, 2), (1, 64)), jnp.float32)
    return {"potential": potential, "start_basis": start_basis}


SIGMA = 0.5
PREC = lax.Precision.HIGHEST

def inner(left, right):
    total = jnp.einsum('kzyx,jzyx->kj', left, right, precision=PREC)
    return total / (left.shape[1] * left.shape[2] * left.shape[3])

def combine(coeff, vectors):
    return jnp.einsum('kj,kzyx->jzyx', coeff, vectors, precision=PREC)

def hamilton(field, potential):
    beside = jnp.roll(field, 1, 1) + jnp.roll(field, -1, 1)
    beside = beside + jnp.roll(field, 1, 2) + jnp.roll(field, -1, 2)
    beside = beside + jnp.roll(field, 1, 3) + jnp.roll(field, -1, 3)
    return potential * field - beside

def orthonormal(block, gram):
    lower = jnp.linalg.cholesky(gram)
    inverse = jax.scipy.linalg.solve_triangular(lower, jnp.eye(gram.shape[0], dtype=jnp.float32), lower=True)
    return combine(inverse.T, block)

def reference(potential, start_basis):
    basis = orthonormal(start_basis, inner(start_basis, start_basis))
    image = hamilton(basis, potential)
    rayleigh = inner(basis, image)
    resid = image - combine(rayleigh, basis)
    shifted = jnp.where(potential >= SIGMA, potential - SIGMA + 6.0, potential - SIGMA - 6.0)
    correction = jnp.zeros_like(basis)
    for sweep in range(NSWEEP):
        coeff = inner(basis, correction)
        proj = correction - combine(coeff, basis)
        moved = hamilton(proj, potential) - SIGMA * proj
        back = inner(basis, moved)
        correction = correction + (-resid - (moved - combine(back, basis))) / shifted
    proj_two = inner(basis, correction)
    fresh = correction - combine(proj_two, basis)
    new_basis = orthonormal(fresh, inner(fresh, fresh))
    return (new_basis, rayleigh)
```

```python
import jax
import jax.numpy as jnp
from jax import lax
from jax.sharding import PartitionSpec as P

NSWEEP = 3


SIGMA = 0.5
PREC = lax.Precision.HIGHEST
AXES = ("space", "vec")


def allsum(x, groups):
    n = lax.axis_size(AXES)
    for group in groups:
        vals = {0: x}
        for m in range(1, 1 << len(group)):
            mask = sum(1 << b for t, b in enumerate(group) if (m >> t) & 1)
            vals[m] = lax.ppermute(x, AXES, [(i, i ^ mask) for i in range(n)])
        for t in range(len(group)):
            vals = {m: vals[m] + vals[m | (1 << t)] for m in vals if not (m >> t) & 1}
        x = vals[0]
    return x


def radix_groups(n):
    bits = n.bit_length() - 1
    order = list(range(bits))
    return [order[i:i + 2] for i in range(0, bits, 2)]


def local_inner(left, right, scale):
    return jnp.einsum("kzyx,jzyx->kj", left, right, precision=PREC) * scale


def combine(coeff, vectors):
    return jnp.einsum("kj,kzyx->jzyx", coeff, vectors, precision=PREC)


def mm(a, b):
    return jnp.matmul(a, b, precision=PREC)


def swap_vec(value):
    return lax.ppermute(value, "vec", [(0, 1), (1, 0)])


def halo(value):
    peers = lax.axis_size("space")
    up = [(i, (i + 1) % peers) for i in range(peers)]
    down = [(j, i) for i, j in up]
    rows = value.shape[2]
    edge = jnp.concatenate([value[:, :, rows - 1:], value[:, :, :1]], axis=2)
    before = lax.ppermute(value, "space", up)
    after = lax.ppermute(value, "space", down)
    ends = swap_vec(edge)
    return before, after, ends


def stencil(value, pieces, potential):
    before, after, ends = pieces
    ext = jnp.concatenate([ends[:, :, :1], value, ends[:, :, 1:]], axis=2)
    beside = before + after
    beside = beside + ext[:, :, :-2] + ext[:, :, 2:]
    beside = beside + jnp.roll(value, 1, 3) + jnp.roll(value, -1, 3)
    return potential * value - beside


def inverse_factor(gram):
    lower = jnp.linalg.cholesky(gram)
    return jax.scipy.linalg.solve_triangular(
        lower, jnp.eye(gram.shape[0], dtype=jnp.float32), lower=True
    )


def local(potential, start_basis):
    mine = start_basis.shape[0]
    rows = start_basis.shape[2] // 2
    v = lax.axis_index("vec")
    groups = radix_groups(lax.axis_size(AXES))
    scale = 1.0 / (
        start_basis.shape[1] * start_basis.shape[2] * start_basis.shape[3] * lax.axis_size("space")
    )
    keep = lax.dynamic_slice_in_dim(start_basis, v * rows, rows, 2)
    give = lax.dynamic_slice_in_dim(start_basis, (1 - v) * rows, rows, 2)
    got = swap_vec(give)
    whole = jnp.where(v == 0, jnp.concatenate([keep, got], 0), jnp.concatenate([got, keep], 0))
    pot = lax.dynamic_slice_in_dim(potential, v * rows, rows, 1)
    shifted = jnp.where(pot >= SIGMA, pot - SIGMA + 6.0, pot - SIGMA - 6.0)

    h_whole = stencil(whole, halo(whole), pot)
    s_d = whole / shifted
    hs_d = h_whole / shifted
    first = allsum(
        jnp.stack(
            [
                local_inner(whole, whole, scale),
                local_inner(whole, h_whole, scale),
                local_inner(whole, s_d, scale),
                local_inner(whole, hs_d, scale),
                local_inner(h_whole, s_d, scale),
                local_inner(h_whole, hs_d, scale),
            ]
        ),
        groups,
    )
    gram, g_sh, u_ss, u_sh, u_hs, u_hh = (first[i] for i in range(6))
    cmat = inverse_factor(gram).T
    ct = cmat.T
    rayleigh = mm(ct, mm(g_sh, cmat))
    b_b = mm(ct, mm(gram, cmat))
    ab_b = mm(ct, mm(g_sh.T, cmat)) - SIGMA * b_b

    basis = combine(cmat, whole)
    image = combine(cmat, h_whole)
    resid = image - combine(rayleigh, basis)
    a_basis = image - SIGMA * basis

    correction = -resid / shifted
    cr = mm(cmat, rayleigh)
    s_rd = mm(u_sh, cmat) - mm(u_ss, cr)
    h_rd = mm(u_hh, cmat) - mm(u_hs, cr)
    coeff = -mm(ct, s_rd)
    ab_c = -mm(ct, h_rd - SIGMA * s_rd)
    back = ab_c - mm(ab_b, coeff)
    proj = correction - combine(coeff, basis)
    moved = stencil(proj, halo(proj), pot) - SIGMA * proj
    correction = correction + (-resid - (moved - combine(back, basis))) / shifted

    for sweep in range(2, NSWEEP):
        pieces = halo(correction)
        red = allsum(
            jnp.stack([local_inner(basis, correction, scale), local_inner(a_basis, correction, scale)]),
            groups,
        )
        coeff = red[0]
        back = red[1] - mm(ab_b, coeff)
        moved = stencil(correction, pieces, pot) - SIGMA * correction - combine(coeff, a_basis)
        correction = correction + (-resid - (moved - combine(back, basis))) / shifted

    proj_two = allsum(local_inner(basis, correction, scale), groups)
    fresh = correction - combine(proj_two, basis)
    gram_two = allsum(local_inner(fresh, fresh, scale), groups)
    new_all = combine(inverse_factor(gram_two).T, fresh)

    own = lax.dynamic_slice_in_dim(new_all, v * mine, mine, 0)
    out = lax.dynamic_slice_in_dim(new_all, (1 - v) * mine, mine, 0)
    back_rows = swap_vec(out)
    new_basis = jnp.where(v == 0, jnp.concatenate([own, back_rows], 2), jnp.concatenate([back_rows, own], 2))
    return (new_basis, rayleigh)


def solution(mesh):
    in_specs = (P("space", None, None), P("vec", "space", None, None))
    out_specs = (P("vec", "space", None, None), P())
    return jax.shard_map(local, mesh=mesh, in_specs=in_specs, out_specs=out_specs, check_vma=False)
```

```python
import jax
import jax.numpy as jnp
from jax import lax
from jax.sharding import PartitionSpec as P

NSWEEP = 3


SIGMA = 0.5
PREC = lax.Precision.HIGHEST
AXES = ("space", "vec")


def allsum(x, groups):
    n = lax.axis_size(AXES)
    for group in groups:
        vals = {0: x}
        for m in range(1, 1 << len(group)):
            mask = sum(1 << b for t, b in enumerate(group) if (m >> t) & 1)
            vals[m] = lax.ppermute(x, AXES, [(i, i ^ mask) for i in range(n)])
        for t in range(len(group)):
            vals = {m: vals[m] + vals[m | (1 << t)] for m in vals if not (m >> t) & 1}
        x = vals[0]
    return x


def radix_groups(n):
    bits = n.bit_length() - 1
    order = list(range(bits))
    return [order[i:i + 2] for i in range(0, bits, 2)]


def local_inner(left, right, scale):
    return jnp.einsum("kzyx,jzyx->kj", left, right, precision=PREC) * scale


def combine(coeff, vectors):
    return jnp.einsum("kj,kzyx->jzyx", coeff, vectors, precision=PREC)


def mm(a, b):
    return jnp.matmul(a, b, precision=PREC)


def swap_vec(value):
    return lax.ppermute(value, "vec", [(0, 1), (1, 0)])


def halo(value):
    peers = lax.axis_size("space")
    up = [(i, (i + 1) % peers) for i in range(peers)]
    down = [(j, i) for i, j in up]
    rows = value.shape[2]
    edge = jnp.concatenate([value[:, :, rows - 1:], value[:, :, :1]], axis=2)
    before = lax.ppermute(value, "space", up)
    after = lax.ppermute(value, "space", down)
    ends = swap_vec(edge)
    return before, after, ends


def stencil(value, pieces, potential):
    before, after, ends = pieces
    ext = jnp.concatenate([ends[:, :, :1], value, ends[:, :, 1:]], axis=2)
    beside = before + after
    beside = beside + ext[:, :, :-2] + ext[:, :, 2:]
    beside = beside + jnp.roll(value, 1, 3) + jnp.roll(value, -1, 3)
    return potential * value - beside


def inverse_factor(gram):
    lower = jnp.linalg.cholesky(gram)
    return jax.scipy.linalg.solve_triangular(
        lower, jnp.eye(gram.shape[0], dtype=jnp.float32), lower=True
    )


def local(potential, start_basis):
    mine = start_basis.shape[0]
    rows = start_basis.shape[2] // 2
    v = lax.axis_index("vec")
    n = lax.axis_size(AXES)
    groups = radix_groups(n)
    scale = 1.0 / (
        start_basis.shape[1] * start_basis.shape[2] * start_basis.shape[3] * lax.axis_size("space")
    )

    def in_order(a, b, axis):
        return jnp.where(v == 0, jnp.concatenate([a, b], axis), jnp.concatenate([b, a], axis))

    ext = jnp.concatenate([start_basis[:, :, -1:], start_basis, start_basis[:, :, :1]], axis=2)
    keep = lax.dynamic_slice_in_dim(ext, v * rows, rows + 2, 2)
    give = lax.dynamic_slice_in_dim(ext, (1 - v) * rows, rows + 2, 2)
    got = swap_vec(give)
    same_up = [(i, (i + 2) % n) for i in range(n)]
    same_down = [(j, i) for i, j in same_up]
    cross_up = [(i, ((i // 2 + 1) * 2 + 1 - i % 2) % n) for i in range(n)]
    cross_down = [(j, i) for i, j in cross_up]
    keep_rows = keep[:, :, 1:-1]
    give_rows = give[:, :, 1:-1]
    before = in_order(lax.ppermute(keep_rows, AXES, same_up), lax.ppermute(give_rows, AXES, cross_up), 0)
    after = in_order(lax.ppermute(keep_rows, AXES, same_down), lax.ppermute(give_rows, AXES, cross_down), 0)
    whole_ext = in_order(keep, got, 0)
    whole = whole_ext[:, :, 1:-1]
    ends = jnp.concatenate([whole_ext[:, :, :1], whole_ext[:, :, -1:]], axis=2)

    pot = lax.dynamic_slice_in_dim(potential, v * rows, rows, 1)
    shifted = jnp.where(pot >= SIGMA, pot - SIGMA + 6.0, pot - SIGMA - 6.0)

    h_whole = stencil(whole, (before, after, ends), pot)
    nb = whole.shape[0]
    fields = jnp.concatenate([whole, h_whole, whole / shifted, h_whole / shifted], 0)
    first = allsum(local_inner(fields[: 2 * nb], fields, scale), groups)
    gram = first[:nb, :nb]
    g_sh = first[:nb, nb:2 * nb]
    u_ss = first[:nb, 2 * nb:3 * nb]
    u_sh = first[:nb, 3 * nb:]
    u_hs = first[nb:, 2 * nb:3 * nb]
    u_hh = first[nb:, 3 * nb:]
    cmat = inverse_factor(gram).T
    ct = cmat.T
    rayleigh = mm(ct, mm(g_sh, cmat))
    b_b = mm(ct, mm(gram, cmat))
    ab_b = mm(ct, mm(g_sh.T, cmat)) - SIGMA * b_b

    basis = combine(cmat, whole)
    image = combine(cmat, h_whole)
    resid = image - combine(rayleigh, basis)
    both = jnp.concatenate([basis, image - SIGMA * basis], 0)
    a_basis = both[nb:]

    correction = -resid / shifted
    cr = mm(cmat, rayleigh)
    s_rd = mm(u_sh, cmat) - mm(u_ss, cr)
    h_rd = mm(u_hh, cmat) - mm(u_hs, cr)
    coeff = -mm(ct, s_rd)
    ab_c = -mm(ct, h_rd - SIGMA * s_rd)
    back = ab_c - mm(ab_b, coeff)
    proj = correction - combine(coeff, basis)
    moved = stencil(proj, halo(proj), pot) - SIGMA * proj
    correction = correction + (-resid - (moved - combine(back, basis))) / shifted

    for sweep in range(2, NSWEEP):
        pieces = halo(correction)
        red = allsum(local_inner(both, correction, scale), groups)
        coeff = red[:nb]
        back = red[nb:] - mm(ab_b, coeff)
        moved = stencil(correction, pieces, pot) - SIGMA * correction - combine(coeff, a_basis)
        correction = correction + (-resid - (moved - combine(back, basis))) / shifted

    red = allsum(
        jnp.concatenate([local_inner(basis, correction, scale), local_inner(correction, correction, scale)], 0),
        groups,
    )
    proj_two = red[:nb]
    gram_two = red[nb:] - 2.0 * mm(proj_two.T, proj_two) + mm(proj_two.T, mm(b_b, proj_two))
    fresh = correction - combine(proj_two, basis)
    new_all = combine(inverse_factor(gram_two).T, fresh)

    own = lax.dynamic_slice_in_dim(new_all, v * mine, mine, 0)
    out = lax.dynamic_slice_in_dim(new_all, (1 - v) * mine, mine, 0)
    new_basis = in_order(own, swap_vec(out), 2)
    return (new_basis, rayleigh)


def solution(mesh):
    in_specs = (P("space", None, None), P("vec", "space", None, None))
    out_specs = (P("vec", "space", None, None), P())
    return jax.shard_map(local, mesh=mesh, in_specs=in_specs, out_specs=out_specs, check_vma=False)
```

```python
import jax
import jax.numpy as jnp
from jax import lax
from jax.sharding import PartitionSpec as P

NSWEEP = 3


SIGMA = 0.5
PREC = lax.Precision.HIGHEST
AXES = ("space", "vec")


def allsum(x, groups):
    n = lax.axis_size(AXES)
    for group in groups:
        vals = {0: x}
        for m in range(1, 1 << len(group)):
            mask = sum(1 << b for t, b in enumerate(group) if (m >> t) & 1)
            vals[m] = lax.ppermute(x, AXES, [(i, i ^ mask) for i in range(n)])
        for t in range(len(group)):
            vals = {m: vals[m] + vals[m | (1 << t)] for m in vals if not (m >> t) & 1}
        x = vals[0]
    return x


def radix_groups(n):
    bits = n.bit_length() - 1
    order = list(range(bits))
    return [order[i:i + 2] for i in range(0, bits, 2)]


def local_inner(left, right, scale):
    return jnp.einsum("kzyx,jzyx->kj", left, right, precision=PREC) * scale


def combine(coeff, vectors):
    return jnp.einsum("kj,kzyx->jzyx", coeff, vectors, precision=PREC)


def mm(a, b):
    return jnp.matmul(a, b, precision=PREC)


def swap_vec(value):
    return lax.ppermute(value, "vec", [(0, 1), (1, 0)])


def halo(value):
    peers = lax.axis_size("space")
    up = [(i, (i + 1) % peers) for i in range(peers)]
    down = [(j, i) for i, j in up]
    rows = value.shape[2]
    edge = jnp.concatenate([value[:, :, rows - 1:], value[:, :, :1]], axis=2)
    before = lax.ppermute(value, "space", up)
    after = lax.ppermute(value, "space", down)
    ends = swap_vec(edge)
    return before, after, ends


def stencil(value, pieces, potential):
    before, after, ends = pieces
    ext = jnp.concatenate([ends[:, :, :1], value, ends[:, :, 1:]], axis=2)
    beside = before + after
    beside = beside + ext[:, :, :-2] + ext[:, :, 2:]
    beside = beside + jnp.roll(value, 1, 3) + jnp.roll(value, -1, 3)
    return potential * value - beside


def inverse_factor(gram):
    lower = jnp.linalg.cholesky(gram)
    return jax.scipy.linalg.solve_triangular(
        lower, jnp.eye(gram.shape[0], dtype=jnp.float32), lower=True
    )


def local(potential, start_basis):
    mine = start_basis.shape[0]
    rows = start_basis.shape[2] // 2
    v = lax.axis_index("vec")
    n = lax.axis_size(AXES)
    groups = radix_groups(n)
    scale = 1.0 / (
        start_basis.shape[1] * start_basis.shape[2] * start_basis.shape[3] * lax.axis_size("space")
    )

    def in_order(a, b, axis):
        return jnp.where(v == 0, jnp.concatenate([a, b], axis), jnp.concatenate([b, a], axis))

    ext = jnp.concatenate([start_basis[:, :, -1:], start_basis, start_basis[:, :, :1]], axis=2)
    keep = lax.dynamic_slice_in_dim(ext, v * rows, rows + 2, 2)
    give = lax.dynamic_slice_in_dim(ext, (1 - v) * rows, rows + 2, 2)
    got = swap_vec(give)
    same_up = [(i, (i + 2) % n) for i in range(n)]
    same_down = [(j, i) for i, j in same_up]
    cross_up = [(i, ((i // 2 + 1) * 2 + 1 - i % 2) % n) for i in range(n)]
    cross_down = [(j, i) for i, j in cross_up]
    keep_rows = keep[:, :, 1:-1]
    give_rows = give[:, :, 1:-1]
    before = in_order(lax.ppermute(keep_rows, AXES, same_up), lax.ppermute(give_rows, AXES, cross_up), 0)
    after = in_order(lax.ppermute(keep_rows, AXES, same_down), lax.ppermute(give_rows, AXES, cross_down), 0)
    whole_ext = in_order(keep, got, 0)
    whole = whole_ext[:, :, 1:-1]
    ends = jnp.concatenate([whole_ext[:, :, :1], whole_ext[:, :, -1:]], axis=2)

    pot = lax.dynamic_slice_in_dim(potential, v * rows, rows, 1)
    pot3 = jnp.concatenate(
        [lax.ppermute(pot, AXES, same_up), pot, lax.ppermute(pot, AXES, same_down)], axis=0
    )
    pot_ends = jnp.concatenate(
        [
            lax.dynamic_slice_in_dim(potential, (v * rows - 1) % (2 * rows), 1, 1),
            lax.dynamic_slice_in_dim(potential, (v * rows + rows) % (2 * rows), 1, 1),
        ],
        axis=1,
    )

    def shift_of(p):
        return jnp.where(p >= SIGMA, p - SIGMA + 6.0, p - SIGMA - 6.0)

    shifted3 = shift_of(pot3)
    shifted = shifted3[1:2]
    shifted_ends = shift_of(pot_ends)

    h_whole = stencil(whole, (before, after, ends), pot)
    h_before = lax.ppermute(h_whole, AXES, same_up)
    h_after = lax.ppermute(h_whole, AXES, same_down)
    h_ends = swap_vec(jnp.concatenate([h_whole[:, :, rows - 1:], h_whole[:, :, :1]], axis=2))
    nb = whole.shape[0]
    fields = jnp.concatenate([whole, h_whole, whole / shifted, h_whole / shifted], 0)
    first = allsum(local_inner(fields[: 2 * nb], fields, scale), groups)
    gram = first[:nb, :nb]
    g_sh = first[:nb, nb:2 * nb]
    u_ss = first[:nb, 2 * nb:3 * nb]
    u_sh = first[:nb, 3 * nb:]
    u_hs = first[nb:, 2 * nb:3 * nb]
    u_hh = first[nb:, 3 * nb:]
    cmat = inverse_factor(gram).T
    ct = cmat.T
    rayleigh = mm(ct, mm(g_sh, cmat))
    b_b = mm(ct, mm(gram, cmat))
    ab_b = mm(ct, mm(g_sh.T, cmat)) - SIGMA * b_b
    cr = mm(cmat, rayleigh)
    s_rd = mm(u_sh, cmat) - mm(u_ss, cr)
    h_rd = mm(u_hh, cmat) - mm(u_hs, cr)
    coeff = -mm(ct, s_rd)
    ab_c = -mm(ct, h_rd - SIGMA * s_rd)
    back = ab_c - mm(ab_b, coeff)

    def first_sweep(s_part, h_part, d_part):
        basis_p = combine(cmat, s_part)
        resid_p = combine(cmat, h_part) - combine(rayleigh, basis_p)
        correction_p = -resid_p / d_part
        return basis_p, resid_p, correction_p, correction_p - combine(coeff, basis_p)

    s3 = jnp.concatenate([before, whole, after], axis=1)
    h3 = jnp.concatenate([h_before, h_whole, h_after], axis=1)
    basis3, resid3, corr3, proj3 = first_sweep(s3, h3, shifted3)
    _, _, _, proj_ends = first_sweep(ends, h_ends, shifted_ends)
    basis, resid, correction, proj = basis3[:, 1:2], resid3[:, 1:2], corr3[:, 1:2], proj3[:, 1:2]
    both = jnp.concatenate([basis, combine(cmat, h_whole) - SIGMA * basis], 0)
    a_basis = both[nb:]

    moved = stencil(proj, (proj3[:, 0:1], proj3[:, 2:3], proj_ends), pot) - SIGMA * proj
    correction = correction + (-resid - (moved - combine(back, basis))) / shifted

    for sweep in range(2, NSWEEP):
        pieces = halo(correction)
        red = allsum(local_inner(both, correction, scale), groups)
        coeff = red[:nb]
        back = red[nb:] - mm(ab_b, coeff)
        moved = stencil(correction, pieces, pot) - SIGMA * correction - combine(coeff, a_basis)
        correction = correction + (-resid - (moved - combine(back, basis))) / shifted

    red = allsum(
        jnp.concatenate([local_inner(basis, correction, scale), local_inner(correction, correction, scale)], 0),
        groups,
    )
    proj_two = red[:nb]
    gram_two = red[nb:] - 2.0 * mm(proj_two.T, proj_two) + mm(proj_two.T, mm(b_b, proj_two))
    fresh = correction - combine(proj_two, basis)
    new_all = combine(inverse_factor(gram_two).T, fresh)

    own = lax.dynamic_slice_in_dim(new_all, v * mine, mine, 0)
    out = lax.dynamic_slice_in_dim(new_all, (1 - v) * mine, mine, 0)
    new_basis = in_order(own, swap_vec(out), 2)
    return (new_basis, rayleigh)


def solution(mesh):
    in_specs = (P("space", None, None), P("vec", "space", None, None))
    out_specs = (P("vec", "space", None, None), P())
    return jax.shard_map(local, mesh=mesh, in_specs=in_specs, out_specs=out_specs, check_vma=False)
```

```python
import jax
import jax.numpy as jnp
from jax import lax
from jax.sharding import PartitionSpec as P

NSWEEP = 3


SIGMA = 0.5
PREC = lax.Precision.HIGHEST
AXES = ("space", "vec")


def allsum(x, groups):
    n = lax.axis_size(AXES)
    for group in groups:
        vals = {0: x}
        for m in range(1, 1 << len(group)):
            mask = sum(1 << b for t, b in enumerate(group) if (m >> t) & 1)
            vals[m] = lax.ppermute(x, AXES, [(i, i ^ mask) for i in range(n)])
        for t in range(len(group)):
            vals = {m: vals[m] + vals[m | (1 << t)] for m in vals if not (m >> t) & 1}
        x = vals[0]
    return x


def radix_groups(n):
    bits = n.bit_length() - 1
    return [[0]] + [list(range(i, min(i + 2, bits))) for i in range(1, bits, 2)]


def local_inner(left, right, scale):
    return jnp.einsum("kzyx,jzyx->kj", left, right, precision=PREC) * scale


def combine(coeff, vectors):
    return jnp.einsum("kj,kzyx->jzyx", coeff, vectors, precision=PREC)


def mm(a, b):
    return jnp.matmul(a, b, precision=PREC)


def swap_vec(value):
    return lax.ppermute(value, "vec", [(0, 1), (1, 0)])


def halo(value):
    peers = lax.axis_size("space")
    up = [(i, (i + 1) % peers) for i in range(peers)]
    down = [(j, i) for i, j in up]
    rows = value.shape[2]
    edge = jnp.concatenate([value[:, :, rows - 1:], value[:, :, :1]], axis=2)
    before = lax.ppermute(value, "space", up)
    after = lax.ppermute(value, "space", down)
    ends = swap_vec(edge)
    return before, after, ends


def stencil(value, pieces, potential):
    before, after, ends = pieces
    ext = jnp.concatenate([ends[:, :, :1], value, ends[:, :, 1:]], axis=2)
    beside = before + after
    beside = beside + ext[:, :, :-2] + ext[:, :, 2:]
    beside = beside + jnp.roll(value, 1, 3) + jnp.roll(value, -1, 3)
    return potential * value - beside


def inverse_factor(gram):
    lower = jnp.linalg.cholesky(gram)
    return jax.scipy.linalg.solve_triangular(
        lower, jnp.eye(gram.shape[0], dtype=jnp.float32), lower=True
    )


def local(potential, start_basis):
    mine = start_basis.shape[0]
    rows = start_basis.shape[2] // 2
    v = lax.axis_index("vec")
    n = lax.axis_size(AXES)
    groups = radix_groups(n)
    scale = 1.0 / (
        start_basis.shape[1] * start_basis.shape[2] * start_basis.shape[3] * lax.axis_size("space")
    )

    def in_order(a, b, axis):
        return jnp.where(v == 0, jnp.concatenate([a, b], axis), jnp.concatenate([b, a], axis))

    ext = jnp.concatenate([start_basis[:, :, -1:], start_basis, start_basis[:, :, :1]], axis=2)
    keep = lax.dynamic_slice_in_dim(ext, v * rows, rows + 2, 2)
    give = lax.dynamic_slice_in_dim(ext, (1 - v) * rows, rows + 2, 2)
    got = swap_vec(give)
    same_up = [(i, (i + 2) % n) for i in range(n)]
    same_down = [(j, i) for i, j in same_up]
    cross_up = [(i, ((i // 2 + 1) * 2 + 1 - i % 2) % n) for i in range(n)]
    cross_down = [(j, i) for i, j in cross_up]
    keep_rows = keep[:, :, 1:-1]
    give_rows = give[:, :, 1:-1]
    before = in_order(lax.ppermute(keep_rows, AXES, same_up), lax.ppermute(give_rows, AXES, cross_up), 0)
    after = in_order(lax.ppermute(keep_rows, AXES, same_down), lax.ppermute(give_rows, AXES, cross_down), 0)
    whole_ext = in_order(keep, got, 0)
    whole = whole_ext[:, :, 1:-1]
    ends = jnp.concatenate([whole_ext[:, :, :1], whole_ext[:, :, -1:]], axis=2)

    pot = lax.dynamic_slice_in_dim(potential, v * rows, rows, 1)
    shifted = jnp.where(pot >= SIGMA, pot - SIGMA + 6.0, pot - SIGMA - 6.0)

    h_whole = stencil(whole, (before, after, ends), pot)
    nb = whole.shape[0]
    fields = jnp.concatenate([whole, h_whole, whole / shifted, h_whole / shifted], 0)
    first = allsum(local_inner(fields[: 2 * nb], fields, scale), groups)
    gram = first[:nb, :nb]
    g_sh = first[:nb, nb:2 * nb]
    u_ss = first[:nb, 2 * nb:3 * nb]
    u_sh = first[:nb, 3 * nb:]
    u_hs = first[nb:, 2 * nb:3 * nb]
    u_hh = first[nb:, 3 * nb:]
    cmat = inverse_factor(gram).T
    ct = cmat.T
    rayleigh = mm(ct, mm(g_sh, cmat))
    b_b = mm(ct, mm(gram, cmat))
    ab_b = mm(ct, mm(g_sh.T, cmat)) - SIGMA * b_b

    basis = combine(cmat, whole)
    image = combine(cmat, h_whole)
    resid = image - combine(rayleigh, basis)
    both = jnp.concatenate([basis, image - SIGMA * basis], 0)
    a_basis = both[nb:]

    correction = -resid / shifted
    cr = mm(cmat, rayleigh)
    s_rd = mm(u_sh, cmat) - mm(u_ss, cr)
    h_rd = mm(u_hh, cmat) - mm(u_hs, cr)
    coeff = -mm(ct, s_rd)
    ab_c = -mm(ct, h_rd - SIGMA * s_rd)
    back = ab_c - mm(ab_b, coeff)
    proj = correction - combine(coeff, basis)
    moved = stencil(proj, halo(proj), pot) - SIGMA * proj
    correction = correction + (-resid - (moved - combine(back, basis))) / shifted

    for sweep in range(2, NSWEEP - 1):
        pieces = halo(correction)
        red = allsum(local_inner(both, correction, scale), groups)
        coeff = red[:nb]
        back = red[nb:] - mm(ab_b, coeff)
        moved = stencil(correction, pieces, pot) - SIGMA * correction - combine(coeff, a_basis)
        correction = correction + (-resid - (moved - combine(back, basis))) / shifted

    a_corr = stencil(correction, halo(correction), pot) - SIGMA * correction
    ys = jnp.concatenate(
        [correction, resid / shifted, a_corr / shifted, a_basis / shifted, basis / shifted], 0
    )
    red = allsum(local_inner(jnp.concatenate([both, ys], 0), ys, scale), groups)
    coeff = red[:nb, :nb]
    back = red[nb:2 * nb, :nb] - mm(ab_b, coeff)
    eye = jnp.eye(nb, dtype=jnp.float32)
    mix = jnp.concatenate([eye, -eye, -eye, coeff, back], 0)
    proj_two = mm(red[:nb], mix)
    c_c = mm(mix.T, mm(red[2 * nb:], mix))
    moved = a_corr - combine(coeff, a_basis)
    correction = correction + (-resid - (moved - combine(back, basis))) / shifted

    gram_two = c_c - 2.0 * mm(proj_two.T, proj_two) + mm(proj_two.T, mm(b_b, proj_two))
    fresh = correction - combine(proj_two, basis)
    new_all = combine(inverse_factor(gram_two).T, fresh)

    own = lax.dynamic_slice_in_dim(new_all, v * mine, mine, 0)
    out = lax.dynamic_slice_in_dim(new_all, (1 - v) * mine, mine, 0)
    new_basis = in_order(own, swap_vec(out), 2)
    return (new_basis, rayleigh)


def solution(mesh):
    in_specs = (P("space", None, None), P("vec", "space", None, None))
    out_specs = (P("vec", "space", None, None), P())
    return jax.shard_map(local, mesh=mesh, in_specs=in_specs, out_specs=out_specs, check_vma=False)
```

```python
import jax
import jax.numpy as jnp
from jax import lax
from jax.sharding import PartitionSpec as P

NSWEEP = 3


SIGMA = 0.5
PREC = lax.Precision.HIGHEST
AXES = ("space", "vec")


def allsum(x, groups):
    n = lax.axis_size(AXES)
    for group in groups:
        vals = {0: x}
        for m in range(1, 1 << len(group)):
            mask = sum(1 << b for t, b in enumerate(group) if (m >> t) & 1)
            vals[m] = lax.ppermute(x, AXES, [(i, i ^ mask) for i in range(n)])
        for t in range(len(group)):
            vals = {m: vals[m] + vals[m | (1 << t)] for m in vals if not (m >> t) & 1}
        x = vals[0]
    return x


def radix_groups(n):
    bits = n.bit_length() - 1
    return [[0]] + [list(range(i, min(i + 2, bits))) for i in range(1, bits, 2)]


def local_inner(left, right, scale):
    return jnp.einsum("kzyx,jzyx->kj", left, right, precision=PREC) * scale


def combine(coeff, vectors):
    return jnp.einsum("kj,kzyx->jzyx", coeff, vectors, precision=PREC)


def mm(a, b):
    return jnp.matmul(a, b, precision=PREC)


def swap_vec(value):
    return lax.ppermute(value, "vec", [(0, 1), (1, 0)])


def halo(value):
    peers = lax.axis_size("space")
    up = [(i, (i + 1) % peers) for i in range(peers)]
    down = [(j, i) for i, j in up]
    rows = value.shape[2]
    edge = jnp.concatenate([value[:, :, rows - 1:], value[:, :, :1]], axis=2)
    before = lax.ppermute(value, "space", up)
    after = lax.ppermute(value, "space", down)
    ends = swap_vec(edge)
    return before, after, ends


def stencil(value, pieces, potential):
    before, after, ends = pieces
    ext = jnp.concatenate([ends[:, :, :1], value, ends[:, :, 1:]], axis=2)
    beside = before + after
    beside = beside + ext[:, :, :-2] + ext[:, :, 2:]
    beside = beside + jnp.roll(value, 1, 3) + jnp.roll(value, -1, 3)
    return potential * value - beside


def inverse_factor(gram):
    lower = jnp.linalg.cholesky(gram)
    return jax.scipy.linalg.solve_triangular(
        lower, jnp.eye(gram.shape[0], dtype=jnp.float32), lower=True
    )


def local(potential, start_basis):
    mine = start_basis.shape[0]
    rows = start_basis.shape[2] // 2
    v = lax.axis_index("vec")
    n = lax.axis_size(AXES)
    groups = radix_groups(n)
    scale = 1.0 / (
        start_basis.shape[1] * start_basis.shape[2] * start_basis.shape[3] * lax.axis_size("space")
    )

    def in_order(a, b, axis):
        return jnp.where(v == 0, jnp.concatenate([a, b], axis), jnp.concatenate([b, a], axis))

    ext = jnp.concatenate([start_basis[:, :, -1:], start_basis, start_basis[:, :, :1]], axis=2)
    keep = lax.dynamic_slice_in_dim(ext, v * rows, rows + 2, 2)
    give = lax.dynamic_slice_in_dim(ext, (1 - v) * rows, rows + 2, 2)
    got = swap_vec(give)
    same_up = [(i, (i + 2) % n) for i in range(n)]
    same_down = [(j, i) for i, j in same_up]
    cross_up = [(i, ((i // 2 + 1) * 2 + 1 - i % 2) % n) for i in range(n)]
    cross_down = [(j, i) for i, j in cross_up]
    keep_rows = keep[:, :, 1:-1]
    give_rows = give[:, :, 1:-1]
    before = in_order(lax.ppermute(keep_rows, AXES, same_up), lax.ppermute(give_rows, AXES, cross_up), 0)
    after = in_order(lax.ppermute(keep_rows, AXES, same_down), lax.ppermute(give_rows, AXES, cross_down), 0)
    whole_ext = in_order(keep, got, 0)
    whole = whole_ext[:, :, 1:-1]
    ends = jnp.concatenate([whole_ext[:, :, :1], whole_ext[:, :, -1:]], axis=2)

    pot = lax.dynamic_slice_in_dim(potential, v * rows, rows, 1)
    shifted = jnp.where(pot >= SIGMA, pot - SIGMA + 6.0, pot - SIGMA - 6.0)

    h_whole = stencil(whole, (before, after, ends), pot)
    nb = whole.shape[0]
    fields = jnp.concatenate([whole, h_whole, whole / shifted, h_whole / shifted], 0)
    first = allsum(local_inner(fields[: 2 * nb], fields, scale), groups)
    gram = first[:nb, :nb]
    g_sh = first[:nb, nb:2 * nb]
    u_ss = first[:nb, 2 * nb:3 * nb]
    u_sh = first[:nb, 3 * nb:]
    u_hs = first[nb:, 2 * nb:3 * nb]
    u_hh = first[nb:, 3 * nb:]
    cmat = inverse_factor(gram).T
    ct = cmat.T
    rayleigh = mm(ct, mm(g_sh, cmat))
    b_b = mm(ct, mm(gram, cmat))
    ab_b = mm(ct, mm(g_sh.T, cmat)) - SIGMA * b_b

    cr = mm(cmat, rayleigh)
    s_rd = mm(u_sh, cmat) - mm(u_ss, cr)
    h_rd = mm(u_hh, cmat) - mm(u_hs, cr)
    coeff = -mm(ct, s_rd)
    ab_c = -mm(ct, h_rd - SIGMA * s_rd)
    back = ab_c - mm(ab_b, coeff)
    zero = jnp.zeros_like(cmat)
    weights = jnp.concatenate(
        [
            jnp.concatenate([cmat, -SIGMA * cmat, -cr, mm(cmat, coeff)], 1),
            jnp.concatenate([zero, cmat, cmat, zero], 1),
        ],
        0,
    )
    parts = combine(weights, jnp.concatenate([whole, h_whole], 0))
    both = parts[: 2 * nb]
    basis, a_basis, resid = parts[:nb], parts[nb:2 * nb], parts[2 * nb:3 * nb]
    correction = -resid / shifted
    proj = correction - parts[3 * nb:]
    pieces = halo(proj)

    moved = stencil(proj, pieces, pot) - SIGMA * proj
    correction = correction + (-resid - (moved - combine(back, basis))) / shifted

    for sweep in range(2, NSWEEP):
        pieces = halo(correction)
        red = allsum(local_inner(both, correction, scale), groups)
        coeff = red[:nb]
        back = red[nb:] - mm(ab_b, coeff)
        moved = stencil(correction, pieces, pot) - SIGMA * correction - combine(coeff, a_basis)
        correction = correction + (-resid - (moved - combine(back, basis))) / shifted

    red = allsum(
        jnp.concatenate([local_inner(basis, correction, scale), local_inner(correction, correction, scale)], 0),
        groups,
    )
    proj_two = red[:nb]
    gram_two = red[nb:] - 2.0 * mm(proj_two.T, proj_two) + mm(proj_two.T, mm(b_b, proj_two))
    fresh = correction - combine(proj_two, basis)
    new_all = combine(inverse_factor(gram_two).T, fresh)

    own = lax.dynamic_slice_in_dim(new_all, v * mine, mine, 0)
    out = lax.dynamic_slice_in_dim(new_all, (1 - v) * mine, mine, 0)
    new_basis = in_order(own, swap_vec(out), 2)
    return (new_basis, rayleigh)


def solution(mesh):
    in_specs = (P("space", None, None), P("vec", "space", None, None))
    out_specs = (P("vec", "space", None, None), P())
    return jax.shard_map(local, mesh=mesh, in_specs=in_specs, out_specs=out_specs, check_vma=False)
```

```python
import jax
import jax.numpy as jnp
from jax import lax
from jax.sharding import PartitionSpec as P

NSWEEP = 3


SIGMA = 0.5
PREC = lax.Precision.HIGHEST
FIELD_PREC = lax.Precision.HIGH
AXES = ("space", "vec")


def allsum(x, groups):
    n = lax.axis_size(AXES)
    for group in groups:
        vals = {0: x}
        for m in range(1, 1 << len(group)):
            mask = sum(1 << b for t, b in enumerate(group) if (m >> t) & 1)
            vals[m] = lax.ppermute(x, AXES, [(i, i ^ mask) for i in range(n)])
        for t in range(len(group)):
            vals = {m: vals[m] + vals[m | (1 << t)] for m in vals if not (m >> t) & 1}
        x = vals[0]
    return x


def radix_groups(n):
    bits = n.bit_length() - 1
    return [[0]] + [list(range(i, min(i + 2, bits))) for i in range(1, bits, 2)]


def local_inner(left, right, scale):
    return jnp.einsum("kzyx,jzyx->kj", left, right, precision=FIELD_PREC) * scale


def combine(coeff, vectors):
    return jnp.einsum("kj,kzyx->jzyx", coeff, vectors, precision=FIELD_PREC)


def mm(a, b):
    return jnp.matmul(a, b, precision=PREC)


def swap_vec(value):
    return lax.ppermute(value, "vec", [(0, 1), (1, 0)])


def halo(value):
    peers = lax.axis_size("space")
    up = [(i, (i + 1) % peers) for i in range(peers)]
    down = [(j, i) for i, j in up]
    rows = value.shape[2]
    edge = jnp.concatenate([value[:, :, rows - 1:], value[:, :, :1]], axis=2)
    before = lax.ppermute(value, "space", up)
    after = lax.ppermute(value, "space", down)
    ends = swap_vec(edge)
    return before, after, ends


def stencil(value, pieces, potential):
    before, after, ends = pieces
    ext = jnp.concatenate([ends[:, :, :1], value, ends[:, :, 1:]], axis=2)
    beside = before + after
    beside = beside + ext[:, :, :-2] + ext[:, :, 2:]
    beside = beside + jnp.roll(value, 1, 3) + jnp.roll(value, -1, 3)
    return potential * value - beside


def inverse_factor(gram):
    lower = jnp.linalg.cholesky(gram)
    return jax.scipy.linalg.solve_triangular(
        lower, jnp.eye(gram.shape[0], dtype=jnp.float32), lower=True
    )


def local(potential, start_basis):
    mine = start_basis.shape[0]
    rows = start_basis.shape[2] // 2
    v = lax.axis_index("vec")
    n = lax.axis_size(AXES)
    groups = radix_groups(n)
    scale = 1.0 / (
        start_basis.shape[1] * start_basis.shape[2] * start_basis.shape[3] * lax.axis_size("space")
    )

    def in_order(a, b, axis):
        return jnp.where(v == 0, jnp.concatenate([a, b], axis), jnp.concatenate([b, a], axis))

    ext = jnp.concatenate([start_basis[:, :, -1:], start_basis, start_basis[:, :, :1]], axis=2)
    keep = lax.dynamic_slice_in_dim(ext, v * rows, rows + 2, 2)
    give = lax.dynamic_slice_in_dim(ext, (1 - v) * rows, rows + 2, 2)
    got = swap_vec(give)
    same_up = [(i, (i + 2) % n) for i in range(n)]
    same_down = [(j, i) for i, j in same_up]
    cross_up = [(i, ((i // 2 + 1) * 2 + 1 - i % 2) % n) for i in range(n)]
    cross_down = [(j, i) for i, j in cross_up]
    keep_rows = keep[:, :, 1:-1]
    give_rows = give[:, :, 1:-1]
    before = in_order(lax.ppermute(keep_rows, AXES, same_up), lax.ppermute(give_rows, AXES, cross_up), 0)
    after = in_order(lax.ppermute(keep_rows, AXES, same_down), lax.ppermute(give_rows, AXES, cross_down), 0)
    whole_ext = in_order(keep, got, 0)
    whole = whole_ext[:, :, 1:-1]
    ends = jnp.concatenate([whole_ext[:, :, :1], whole_ext[:, :, -1:]], axis=2)

    pot = lax.dynamic_slice_in_dim(potential, v * rows, rows, 1)
    shifted = jnp.where(pot >= SIGMA, pot - SIGMA + 6.0, pot - SIGMA - 6.0)

    h_whole = stencil(whole, (before, after, ends), pot)
    nb = whole.shape[0]
    fields = jnp.concatenate([whole, h_whole, whole / shifted, h_whole / shifted], 0)
    first = allsum(local_inner(fields[: 2 * nb], fields, scale), groups)
    gram = first[:nb, :nb]
    g_sh = first[:nb, nb:2 * nb]
    u_ss = first[:nb, 2 * nb:3 * nb]
    u_sh = first[:nb, 3 * nb:]
    u_hs = first[nb:, 2 * nb:3 * nb]
    u_hh = first[nb:, 3 * nb:]
    cmat = inverse_factor(gram).T
    ct = cmat.T
    rayleigh = mm(ct, mm(g_sh, cmat))
    b_b = mm(ct, mm(gram, cmat))
    ab_b = mm(ct, mm(g_sh.T, cmat)) - SIGMA * b_b

    cr = mm(cmat, rayleigh)
    s_rd = mm(u_sh, cmat) - mm(u_ss, cr)
    h_rd = mm(u_hh, cmat) - mm(u_hs, cr)
    coeff = -mm(ct, s_rd)
    ab_c = -mm(ct, h_rd - SIGMA * s_rd)
    back = ab_c - mm(ab_b, coeff)
    zero = jnp.zeros_like(cmat)
    weights = jnp.concatenate(
        [
            jnp.concatenate([cmat, -SIGMA * cmat, -cr, mm(cmat, coeff)], 1),
            jnp.concatenate([zero, cmat, cmat, zero], 1),
        ],
        0,
    )
    parts = combine(weights, jnp.concatenate([whole, h_whole], 0))
    both = parts[: 2 * nb]
    basis, a_basis, resid = parts[:nb], parts[nb:2 * nb], parts[2 * nb:3 * nb]
    correction = -resid / shifted
    proj = correction - parts[3 * nb:]
    pieces = halo(proj)

    moved = stencil(proj, pieces, pot) - SIGMA * proj
    correction = correction + (-resid - (moved - combine(back, basis))) / shifted

    for sweep in range(2, NSWEEP):
        pieces = halo(correction)
        red = allsum(local_inner(both, correction, scale), groups)
        coeff = red[:nb]
        back = red[nb:] - mm(ab_b, coeff)
        moved = stencil(correction, pieces, pot) - SIGMA * correction - combine(coeff, a_basis)
        correction = correction + (-resid - (moved - combine(back, basis))) / shifted

    red = allsum(
        jnp.concatenate([local_inner(basis, correction, scale), local_inner(correction, correction, scale)], 0),
        groups,
    )
    proj_two = red[:nb]
    gram_two = red[nb:] - 2.0 * mm(proj_two.T, proj_two) + mm(proj_two.T, mm(b_b, proj_two))
    fresh = correction - combine(proj_two, basis)
    new_all = combine(inverse_factor(gram_two).T, fresh)

    own = lax.dynamic_slice_in_dim(new_all, v * mine, mine, 0)
    out = lax.dynamic_slice_in_dim(new_all, (1 - v) * mine, mine, 0)
    new_basis = in_order(own, swap_vec(out), 2)
    return (new_basis, rayleigh)


def solution(mesh):
    in_specs = (P("space", None, None), P("vec", "space", None, None))
    out_specs = (P("vec", "space", None, None), P())
    return jax.shard_map(local, mesh=mesh, in_specs=in_specs, out_specs=out_specs, check_vma=False)
```

```python
import jax
import jax.numpy as jnp
from jax import lax
from jax.sharding import PartitionSpec as P

NSWEEP = 3


SIGMA = 0.5
PREC = lax.Precision.HIGHEST
FIELD_PREC = lax.Precision.HIGH
AXES = ("space", "vec")


def allsum(x, groups):
    n = lax.axis_size(AXES)
    for group in groups:
        vals = {0: x}
        for m in range(1, 1 << len(group)):
            mask = sum(1 << b for t, b in enumerate(group) if (m >> t) & 1)
            vals[m] = lax.ppermute(x, AXES, [(i, i ^ mask) for i in range(n)])
        for t in range(len(group)):
            vals = {m: vals[m] + vals[m | (1 << t)] for m in vals if not (m >> t) & 1}
        x = vals[0]
    return x


def radix_groups(n):
    bits = n.bit_length() - 1
    return [[0]] + [list(range(i, min(i + 2, bits))) for i in range(1, bits, 2)]


def local_inner(left, right, scale):
    return jnp.einsum("kzyx,jzyx->kj", left, right, precision=FIELD_PREC) * scale


def combine(coeff, vectors):
    return jnp.einsum("kj,kzyx->jzyx", coeff, vectors, precision=FIELD_PREC)


def mm(a, b):
    return jnp.matmul(a, b, precision=PREC)


def swap_vec(value):
    return lax.ppermute(value, "vec", [(0, 1), (1, 0)])


def halo(value):
    peers = lax.axis_size("space")
    up = [(i, (i + 1) % peers) for i in range(peers)]
    down = [(j, i) for i, j in up]
    rows = value.shape[2]
    edge = jnp.concatenate([value[:, :, rows - 1:], value[:, :, :1]], axis=2)
    before = lax.ppermute(value, "space", up)
    after = lax.ppermute(value, "space", down)
    ends = swap_vec(edge)
    return before, after, ends


def stencil(value, pieces, potential):
    before, after, ends = pieces
    ext = jnp.concatenate([ends[:, :, :1], value, ends[:, :, 1:]], axis=2)
    beside = before + after
    beside = beside + ext[:, :, :-2] + ext[:, :, 2:]
    beside = beside + jnp.roll(value, 1, 3) + jnp.roll(value, -1, 3)
    return potential * value - beside


def inverse_factor(gram):
    lower = jnp.linalg.cholesky(gram)
    return jax.scipy.linalg.solve_triangular(
        lower, jnp.eye(gram.shape[0], dtype=jnp.float32), lower=True
    )


def local(potential, start_basis):
    mine = start_basis.shape[0]
    rows = start_basis.shape[2] // 2
    v = lax.axis_index("vec")
    n = lax.axis_size(AXES)
    groups = radix_groups(n)
    scale = 1.0 / (
        start_basis.shape[1] * start_basis.shape[2] * start_basis.shape[3] * lax.axis_size("space")
    )

    def in_order(a, b, axis):
        return jnp.where(v == 0, jnp.concatenate([a, b], axis), jnp.concatenate([b, a], axis))

    ext = jnp.concatenate([start_basis[:, :, -1:], start_basis, start_basis[:, :, :1]], axis=2)
    keep = lax.dynamic_slice_in_dim(ext, v * rows, rows + 2, 2)
    give = lax.dynamic_slice_in_dim(ext, (1 - v) * rows, rows + 2, 2)
    got = swap_vec(give)
    same_up = [(i, (i + 2) % n) for i in range(n)]
    same_down = [(j, i) for i, j in same_up]
    cross_up = [(i, ((i // 2 + 1) * 2 + 1 - i % 2) % n) for i in range(n)]
    cross_down = [(j, i) for i, j in cross_up]
    keep_rows = keep[:, :, 1:-1]
    give_rows = give[:, :, 1:-1]
    before = in_order(lax.ppermute(keep_rows, AXES, same_up), lax.ppermute(give_rows, AXES, cross_up), 0)
    after = in_order(lax.ppermute(keep_rows, AXES, same_down), lax.ppermute(give_rows, AXES, cross_down), 0)
    whole_ext = in_order(keep, got, 0)
    whole = whole_ext[:, :, 1:-1]
    ends = jnp.concatenate([whole_ext[:, :, :1], whole_ext[:, :, -1:]], axis=2)

    pot = lax.dynamic_slice_in_dim(potential, v * rows, rows, 1)
    shifted = jnp.where(pot >= SIGMA, pot - SIGMA + 6.0, pot - SIGMA - 6.0)

    h_whole = stencil(whole, (before, after, ends), pot)
    nb = whole.shape[0]
    fields = jnp.concatenate([whole, h_whole, whole / shifted, h_whole / shifted], 0)
    first = allsum(local_inner(fields[: 2 * nb], fields, scale), groups)
    gram = first[:nb, :nb]
    g_sh = first[:nb, nb:2 * nb]
    u_ss = first[:nb, 2 * nb:3 * nb]
    u_sh = first[:nb, 3 * nb:]
    u_hs = first[nb:, 2 * nb:3 * nb]
    u_hh = first[nb:, 3 * nb:]
    cmat = inverse_factor(gram).T
    ct = cmat.T
    rayleigh = mm(ct, mm(g_sh, cmat))
    b_b = mm(ct, mm(gram, cmat))
    ab_b = mm(ct, mm(g_sh.T, cmat)) - SIGMA * b_b

    cr = mm(cmat, rayleigh)
    s_rd = mm(u_sh, cmat) - mm(u_ss, cr)
    h_rd = mm(u_hh, cmat) - mm(u_hs, cr)
    coeff = -mm(ct, s_rd)
    ab_c = -mm(ct, h_rd - SIGMA * s_rd)
    back = ab_c - mm(ab_b, coeff)
    zero = jnp.zeros_like(cmat)
    weights = jnp.concatenate(
        [
            jnp.concatenate([cmat, -SIGMA * cmat, -cr, mm(cmat, coeff)], 1),
            jnp.concatenate([zero, cmat, cmat, zero], 1),
        ],
        0,
    )
    parts = combine(weights, jnp.concatenate([whole, h_whole], 0))
    both = parts[: 2 * nb]
    basis, a_basis, resid = parts[:nb], parts[nb:2 * nb], parts[2 * nb:3 * nb]
    correction = -resid / shifted
    proj = correction - parts[3 * nb:]
    pieces = halo(proj)

    moved = stencil(proj, pieces, pot) - SIGMA * proj
    correction = correction + (-resid - (moved - combine(back, basis))) / shifted

    for sweep in range(2, NSWEEP - 1):
        pieces = halo(correction)
        red = allsum(local_inner(both, correction, scale), groups)
        coeff = red[:nb]
        back = red[nb:] - mm(ab_b, coeff)
        moved = stencil(correction, pieces, pot) - SIGMA * correction - combine(coeff, a_basis)
        correction = correction + (-resid - (moved - combine(back, basis))) / shifted

    pieces = halo(correction)
    y_pre = jnp.concatenate([correction, resid / shifted, a_basis / shifted, basis / shifted], 0)
    x_pre = jnp.concatenate([both, y_pre], 0)
    g_pre = local_inner(x_pre, y_pre, scale)
    a_corr = stencil(correction, pieces, pot) - SIGMA * correction
    y_a = a_corr / shifted
    g_a = local_inner(x_pre, y_a, scale)
    g_aa = local_inner(y_a, y_a, scale)
    width = y_pre.shape[0]
    packed = jnp.concatenate(
        [
            jnp.concatenate([g_pre, g_a], 1),
            jnp.concatenate([jnp.zeros((nb, width), jnp.float32), g_aa], 1),
        ],
        0,
    )
    red = allsum(packed, groups)
    b_y = red[:nb]
    coeff = b_y[:, :nb]
    back = red[nb:2 * nb, :nb] - mm(ab_b, coeff)
    y_rows = red[2 * nb:2 * nb + width]
    y_y = jnp.concatenate(
        [y_rows, jnp.concatenate([y_rows[:, width:].T, red[2 * nb + width:, width:]], 1)], 0
    )
    eye = jnp.eye(nb, dtype=jnp.float32)
    mix = jnp.concatenate([eye, -eye, coeff, back, -eye], 0)
    proj_two = mm(b_y, mix)
    c_c = mm(mix.T, mm(y_y, mix))
    moved = a_corr - combine(coeff, a_basis)
    correction = correction + (-resid - (moved - combine(back, basis))) / shifted

    gram_two = c_c - 2.0 * mm(proj_two.T, proj_two) + mm(proj_two.T, mm(b_b, proj_two))
    fresh = correction - combine(proj_two, basis)
    new_all = combine(inverse_factor(gram_two).T, fresh)

    own = lax.dynamic_slice_in_dim(new_all, v * mine, mine, 0)
    out = lax.dynamic_slice_in_dim(new_all, (1 - v) * mine, mine, 0)
    new_basis = in_order(own, swap_vec(out), 2)
    return (new_basis, rayleigh)


def solution(mesh):
    in_specs = (P("space", None, None), P("vec", "space", None, None))
    out_specs = (P("vec", "space", None, None), P())
    return jax.shard_map(local, mesh=mesh, in_specs=in_specs, out_specs=out_specs, check_vma=False)
```

```python
import jax
import jax.numpy as jnp
from jax import lax
from jax.sharding import PartitionSpec as P

NSWEEP = 3


SIGMA = 0.5
PREC = lax.Precision.HIGHEST
FIELD_PREC = lax.Precision.HIGH
AXES = ("space", "vec")


def allsum(x, groups):
    n = lax.axis_size(AXES)
    for group in groups:
        vals = {0: x}
        for m in range(1, 1 << len(group)):
            mask = sum(1 << b for t, b in enumerate(group) if (m >> t) & 1)
            vals[m] = lax.ppermute(x, AXES, [(i, i ^ mask) for i in range(n)])
        for t in range(len(group)):
            vals = {m: vals[m] + vals[m | (1 << t)] for m in vals if not (m >> t) & 1}
        x = vals[0]
    return x


def radix_groups(n):
    bits = n.bit_length() - 1
    return [[0]] + [list(range(i, min(i + 2, bits))) for i in range(1, bits, 2)]


def local_inner(left, right, scale):
    return jnp.einsum("kzyx,jzyx->kj", left, right, precision=FIELD_PREC) * scale


def combine(coeff, vectors):
    return jnp.einsum("kj,kzyx->jzyx", coeff, vectors, precision=FIELD_PREC)


def mm(a, b):
    return jnp.matmul(a, b, precision=PREC)


def swap_vec(value):
    return lax.ppermute(value, "vec", [(0, 1), (1, 0)])


def halo(value):
    peers = lax.axis_size("space")
    up = [(i, (i + 1) % peers) for i in range(peers)]
    down = [(j, i) for i, j in up]
    rows = value.shape[2]
    edge = jnp.concatenate([value[:, :, rows - 1:], value[:, :, :1]], axis=2)
    before = lax.ppermute(value, "space", up)
    after = lax.ppermute(value, "space", down)
    ends = swap_vec(edge)
    return before, after, ends


def stencil(value, pieces, potential):
    before, after, ends = pieces
    ext = jnp.concatenate([ends[:, :, :1], value, ends[:, :, 1:]], axis=2)
    beside = before + after
    beside = beside + ext[:, :, :-2] + ext[:, :, 2:]
    beside = beside + jnp.roll(value, 1, 3) + jnp.roll(value, -1, 3)
    return potential * value - beside


def inverse_factor(gram):
    lower = jnp.linalg.cholesky(gram)
    return jax.scipy.linalg.solve_triangular(
        lower, jnp.eye(gram.shape[0], dtype=jnp.float32), lower=True
    )


def local(potential, start_basis):
    mine = start_basis.shape[0]
    rows = start_basis.shape[2] // 2
    v = lax.axis_index("vec")
    n = lax.axis_size(AXES)
    groups = radix_groups(n)
    scale = 1.0 / (
        start_basis.shape[1] * start_basis.shape[2] * start_basis.shape[3] * lax.axis_size("space")
    )

    def in_order(a, b, axis):
        return jnp.where(v == 0, jnp.concatenate([a, b], axis), jnp.concatenate([b, a], axis))

    ext = jnp.concatenate([start_basis[:, :, -1:], start_basis, start_basis[:, :, :1]], axis=2)
    keep = lax.dynamic_slice_in_dim(ext, v * rows, rows + 2, 2)
    give = lax.dynamic_slice_in_dim(ext, (1 - v) * rows, rows + 2, 2)
    got = swap_vec(give)
    same_up = [(i, (i + 2) % n) for i in range(n)]
    same_down = [(j, i) for i, j in same_up]
    cross_up = [(i, ((i // 2 + 1) * 2 + 1 - i % 2) % n) for i in range(n)]
    cross_down = [(j, i) for i, j in cross_up]
    keep_rows = keep[:, :, 1:-1]
    give_rows = give[:, :, 1:-1]
    pot = lax.dynamic_slice_in_dim(potential, v * rows, rows, 1)
    keep_pot = jnp.concatenate([keep_rows, pot[None]], 0)
    up_same = lax.ppermute(keep_pot, AXES, same_up)
    down_same = lax.ppermute(keep_pot, AXES, same_down)
    before = in_order(up_same[:mine], lax.ppermute(give_rows, AXES, cross_up), 0)
    after = in_order(down_same[:mine], lax.ppermute(give_rows, AXES, cross_down), 0)
    pot_nb = jnp.concatenate([up_same[mine], down_same[mine]], 0)
    pot_ends = jnp.concatenate(
        [
            lax.dynamic_slice_in_dim(potential, (v * rows - 1) % (2 * rows), 1, 1),
            lax.dynamic_slice_in_dim(potential, (v * rows + rows) % (2 * rows), 1, 1),
        ],
        axis=1,
    )
    whole_ext = in_order(keep, got, 0)
    whole = whole_ext[:, :, 1:-1]
    ends = jnp.concatenate([whole_ext[:, :, :1], whole_ext[:, :, -1:]], axis=2)

    def shift_of(p):
        return jnp.where(p >= SIGMA, p - SIGMA + 6.0, p - SIGMA - 6.0)

    shifted = shift_of(pot)

    h_whole = stencil(whole, (before, after, ends), pot)
    h_nb = jnp.concatenate(
        [lax.ppermute(h_whole, AXES, same_up), lax.ppermute(h_whole, AXES, same_down)], axis=1
    )
    h_ends = swap_vec(jnp.concatenate([h_whole[:, :, rows - 1:], h_whole[:, :, :1]], axis=2))
    nb = whole.shape[0]
    fields = jnp.concatenate([whole, h_whole, whole / shifted, h_whole / shifted], 0)
    first = allsum(local_inner(fields[: 2 * nb], fields, scale), groups)
    gram = first[:nb, :nb]
    g_sh = first[:nb, nb:2 * nb]
    u_ss = first[:nb, 2 * nb:3 * nb]
    u_sh = first[:nb, 3 * nb:]
    u_hs = first[nb:, 2 * nb:3 * nb]
    u_hh = first[nb:, 3 * nb:]
    cmat = inverse_factor(gram).T
    ct = cmat.T
    rayleigh = mm(ct, mm(g_sh, cmat))
    b_b = mm(ct, mm(gram, cmat))
    ab_b = mm(ct, mm(g_sh.T, cmat)) - SIGMA * b_b

    cr = mm(cmat, rayleigh)
    s_rd = mm(u_sh, cmat) - mm(u_ss, cr)
    h_rd = mm(u_hh, cmat) - mm(u_hs, cr)
    coeff = -mm(ct, s_rd)
    ab_c = -mm(ct, h_rd - SIGMA * s_rd)
    back = ab_c - mm(ab_b, coeff)
    zero = jnp.zeros_like(cmat)
    weights = jnp.concatenate(
        [
            jnp.concatenate([cmat, -SIGMA * cmat, -cr, mm(cmat, coeff)], 1),
            jnp.concatenate([zero, cmat, cmat, zero], 1),
        ],
        0,
    )
    parts = combine(weights, jnp.concatenate([whole, h_whole], 0))
    both = parts[: 2 * nb]
    basis, a_basis, resid = parts[:nb], parts[nb:2 * nb], parts[2 * nb:3 * nb]
    correction = -resid / shifted
    proj = correction - parts[3 * nb:]
    w_nb = weights[:, 2 * nb:]

    def proj_of(s_part, h_part, d_part):
        got = combine(w_nb, jnp.concatenate([s_part, h_part], 0))
        return -got[:nb] / d_part - got[nb:]

    proj_nb = proj_of(jnp.concatenate([before, after], axis=1), h_nb, shift_of(pot_nb))
    proj_ends = proj_of(ends, h_ends, shift_of(pot_ends))
    pieces = (proj_nb[:, 0:1], proj_nb[:, 1:2], proj_ends)

    moved = stencil(proj, pieces, pot) - SIGMA * proj
    correction = correction + (-resid - (moved - combine(back, basis))) / shifted

    for sweep in range(2, NSWEEP):
        pieces = halo(correction)
        red = allsum(local_inner(both, correction, scale), groups)
        coeff = red[:nb]
        back = red[nb:] - mm(ab_b, coeff)
        moved = stencil(correction, pieces, pot) - SIGMA * correction - combine(coeff, a_basis)
        correction = correction + (-resid - (moved - combine(back, basis))) / shifted

    red = allsum(
        jnp.concatenate([local_inner(basis, correction, scale), local_inner(correction, correction, scale)], 0),
        groups,
    )
    proj_two = red[:nb]
    gram_two = red[nb:] - 2.0 * mm(proj_two.T, proj_two) + mm(proj_two.T, mm(b_b, proj_two))
    fresh = correction - combine(proj_two, basis)
    new_all = combine(inverse_factor(gram_two).T, fresh)

    own = lax.dynamic_slice_in_dim(new_all, v * mine, mine, 0)
    out = lax.dynamic_slice_in_dim(new_all, (1 - v) * mine, mine, 0)
    new_basis = in_order(own, swap_vec(out), 2)
    return (new_basis, rayleigh)


def solution(mesh):
    in_specs = (P("space", None, None), P("vec", "space", None, None))
    out_specs = (P("vec", "space", None, None), P())
    return jax.shard_map(local, mesh=mesh, in_specs=in_specs, out_specs=out_specs, check_vma=False)
```

```python
import jax
import jax.numpy as jnp
from jax import lax
from jax.sharding import PartitionSpec as P

NSWEEP = 3


SIGMA = 0.5
PREC = lax.Precision.HIGHEST
FIELD_PREC = lax.Precision.HIGH
AXES = ("space", "vec")


def allsum(x, groups):
    n = lax.axis_size(AXES)
    for group in groups:
        vals = {0: x}
        for m in range(1, 1 << len(group)):
            mask = sum(1 << b for t, b in enumerate(group) if (m >> t) & 1)
            vals[m] = lax.ppermute(x, AXES, [(i, i ^ mask) for i in range(n)])
        for t in range(len(group)):
            vals = {m: vals[m] + vals[m | (1 << t)] for m in vals if not (m >> t) & 1}
        x = vals[0]
    return x


def radix_groups(n):
    bits = n.bit_length() - 1
    return [[0]] + [list(range(i, min(i + 2, bits))) for i in range(1, bits, 2)]


def local_inner(left, right, scale):
    return jnp.einsum("kzyx,jzyx->kj", left, right, precision=FIELD_PREC) * scale


def combine(coeff, vectors):
    return jnp.einsum("kj,kzyx->jzyx", coeff, vectors, precision=FIELD_PREC)


def mm(a, b):
    return jnp.matmul(a, b, precision=PREC)


def swap_vec(value):
    return lax.ppermute(value, "vec", [(0, 1), (1, 0)])


def halo(value):
    peers = lax.axis_size("space")
    up = [(i, (i + 1) % peers) for i in range(peers)]
    down = [(j, i) for i, j in up]
    rows = value.shape[2]
    edge = jnp.concatenate([value[:, :, rows - 1:], value[:, :, :1]], axis=2)
    half = value.shape[0] // 2
    before = jnp.concatenate(
        [lax.ppermute(value[:half], "space", up), lax.ppermute(value[half:], "space", up)], 0
    )
    after = jnp.concatenate(
        [lax.ppermute(value[:half], "space", down), lax.ppermute(value[half:], "space", down)], 0
    )
    ends = swap_vec(edge)
    return before, after, ends


def stencil(value, pieces, potential):
    before, after, ends = pieces
    ext = jnp.concatenate([ends[:, :, :1], value, ends[:, :, 1:]], axis=2)
    beside = before + after
    beside = beside + ext[:, :, :-2] + ext[:, :, 2:]
    beside = beside + jnp.roll(value, 1, 3) + jnp.roll(value, -1, 3)
    return potential * value - beside


def inverse_factor(gram):
    lower = jnp.linalg.cholesky(gram)
    return jax.scipy.linalg.solve_triangular(
        lower, jnp.eye(gram.shape[0], dtype=jnp.float32), lower=True
    )


def local(potential, start_basis):
    mine = start_basis.shape[0]
    rows = start_basis.shape[2] // 2
    v = lax.axis_index("vec")
    n = lax.axis_size(AXES)
    groups = radix_groups(n)
    scale = 1.0 / (
        start_basis.shape[1] * start_basis.shape[2] * start_basis.shape[3] * lax.axis_size("space")
    )

    def in_order(a, b, axis):
        return jnp.where(v == 0, jnp.concatenate([a, b], axis), jnp.concatenate([b, a], axis))

    ext = jnp.concatenate([start_basis[:, :, -1:], start_basis, start_basis[:, :, :1]], axis=2)
    keep = lax.dynamic_slice_in_dim(ext, v * rows, rows + 2, 2)
    give = lax.dynamic_slice_in_dim(ext, (1 - v) * rows, rows + 2, 2)
    got = swap_vec(give)
    same_up = [(i, (i + 2) % n) for i in range(n)]
    same_down = [(j, i) for i, j in same_up]
    cross_up = [(i, ((i // 2 + 1) * 2 + 1 - i % 2) % n) for i in range(n)]
    cross_down = [(j, i) for i, j in cross_up]
    keep_rows = keep[:, :, 1:-1]
    give_rows = give[:, :, 1:-1]
    before = in_order(lax.ppermute(keep_rows, AXES, same_up), lax.ppermute(give_rows, AXES, cross_up), 0)
    after = in_order(lax.ppermute(keep_rows, AXES, same_down), lax.ppermute(give_rows, AXES, cross_down), 0)
    whole_ext = in_order(keep, got, 0)
    whole = whole_ext[:, :, 1:-1]
    ends = jnp.concatenate([whole_ext[:, :, :1], whole_ext[:, :, -1:]], axis=2)

    pot = lax.dynamic_slice_in_dim(potential, v * rows, rows, 1)
    shifted = jnp.where(pot >= SIGMA, pot - SIGMA + 6.0, pot - SIGMA - 6.0)

    h_whole = stencil(whole, (before, after, ends), pot)
    nb = whole.shape[0]
    fields = jnp.concatenate([whole, h_whole, whole / shifted, h_whole / shifted], 0)
    first = allsum(local_inner(fields[: 2 * nb], fields, scale), groups)
    gram = first[:nb, :nb]
    g_sh = first[:nb, nb:2 * nb]
    u_ss = first[:nb, 2 * nb:3 * nb]
    u_sh = first[:nb, 3 * nb:]
    u_hs = first[nb:, 2 * nb:3 * nb]
    u_hh = first[nb:, 3 * nb:]
    cmat = inverse_factor(gram).T
    ct = cmat.T
    rayleigh = mm(ct, mm(g_sh, cmat))
    b_b = mm(ct, mm(gram, cmat))
    ab_b = mm(ct, mm(g_sh.T, cmat)) - SIGMA * b_b

    cr = mm(cmat, rayleigh)
    s_rd = mm(u_sh, cmat) - mm(u_ss, cr)
    h_rd = mm(u_hh, cmat) - mm(u_hs, cr)
    coeff = -mm(ct, s_rd)
    ab_c = -mm(ct, h_rd - SIGMA * s_rd)
    back = ab_c - mm(ab_b, coeff)
    zero = jnp.zeros_like(cmat)
    weights = jnp.concatenate(
        [
            jnp.concatenate([cmat, -SIGMA * cmat, -cr, mm(cmat, coeff)], 1),
            jnp.concatenate([zero, cmat, cmat, zero], 1),
        ],
        0,
    )
    parts = combine(weights, jnp.concatenate([whole, h_whole], 0))
    both = parts[: 2 * nb]
    basis, a_basis, resid = parts[:nb], parts[nb:2 * nb], parts[2 * nb:3 * nb]
    correction = -resid / shifted
    proj = correction - parts[3 * nb:]
    pieces = halo(proj)

    moved = stencil(proj, pieces, pot) - SIGMA * proj
    correction = correction + (-resid - (moved - combine(back, basis))) / shifted

    for sweep in range(2, NSWEEP):
        pieces = halo(correction)
        red = allsum(local_inner(both, correction, scale), groups)
        coeff = red[:nb]
        back = red[nb:] - mm(ab_b, coeff)
        moved = stencil(correction, pieces, pot) - SIGMA * correction - combine(coeff, a_basis)
        correction = correction + (-resid - (moved - combine(back, basis))) / shifted

    red = allsum(
        jnp.concatenate([local_inner(basis, correction, scale), local_inner(correction, correction, scale)], 0),
        groups,
    )
    proj_two = red[:nb]
    gram_two = red[nb:] - 2.0 * mm(proj_two.T, proj_two) + mm(proj_two.T, mm(b_b, proj_two))
    fresh = correction - combine(proj_two, basis)
    new_all = combine(inverse_factor(gram_two).T, fresh)

    own = lax.dynamic_slice_in_dim(new_all, v * mine, mine, 0)
    out = lax.dynamic_slice_in_dim(new_all, (1 - v) * mine, mine, 0)
    half = mine // 2
    new_basis = in_order(own, jnp.concatenate([swap_vec(out[:half]), swap_vec(out[half:])], 0), 2)
    return (new_basis, rayleigh)


def solution(mesh):
    in_specs = (P("space", None, None), P("vec", "space", None, None))
    out_specs = (P("vec", "space", None, None), P())
    return jax.shard_map(local, mesh=mesh, in_specs=in_specs, out_specs=out_specs, check_vma=False)
```

```python
import jax
import jax.numpy as jnp
from jax import lax
from jax.experimental import pallas as pl
from jax.experimental.pallas import tpu as pltpu
from jax.sharding import PartitionSpec as P

NSWEEP = 3


SIGMA = 0.5
PREC = lax.Precision.HIGHEST
FIELD_PREC = lax.Precision.HIGH
AXES = ("space", "vec")


def allsum(x, groups):
    n = lax.axis_size(AXES)
    for group in groups:
        vals = {0: x}
        for m in range(1, 1 << len(group)):
            mask = sum(1 << b for t, b in enumerate(group) if (m >> t) & 1)
            vals[m] = lax.ppermute(x, AXES, [(i, i ^ mask) for i in range(n)])
        for t in range(len(group)):
            vals = {m: vals[m] + vals[m | (1 << t)] for m in vals if not (m >> t) & 1}
        x = vals[0]
    return x


def radix_groups(n):
    bits = n.bit_length() - 1
    return [[0]] + [list(range(i, min(i + 2, bits))) for i in range(1, bits, 2)]


def local_inner(left, right, scale):
    return jnp.einsum("kzyx,jzyx->kj", left, right, precision=FIELD_PREC) * scale


def combine(coeff, vectors):
    return jnp.einsum("kj,kzyx->jzyx", coeff, vectors, precision=FIELD_PREC)


def mm(a, b):
    return jnp.matmul(a, b, precision=PREC)


def swap_vec(value):
    return lax.ppermute(value, "vec", [(0, 1), (1, 0)])


def halo(value):
    peers = lax.axis_size("space")
    up = [(i, (i + 1) % peers) for i in range(peers)]
    down = [(j, i) for i, j in up]
    rows = value.shape[2]
    edge = jnp.concatenate([value[:, :, rows - 1:], value[:, :, :1]], axis=2)
    before = lax.ppermute(value, "space", up)
    after = lax.ppermute(value, "space", down)
    ends = swap_vec(edge)
    return before, after, ends


def stencil(value, pieces, potential):
    before, after, ends = pieces
    ext = jnp.concatenate([ends[:, :, :1], value, ends[:, :, 1:]], axis=2)
    beside = before + after
    beside = beside + ext[:, :, :-2] + ext[:, :, 2:]
    beside = beside + jnp.roll(value, 1, 3) + jnp.roll(value, -1, 3)
    return potential * value - beside


def _upper_inverse_kernel(a_ref, c_ref):
    n = a_ref.shape[0]
    a = a_ref[...]
    rows = lax.broadcasted_iota(jnp.int32, (n, n), 0)
    cols = lax.broadcasted_iota(jnp.int32, (n, n), 1)
    colv = lax.broadcasted_iota(jnp.int32, (n, 1), 0)
    lcols, diags = [], []
    for j in range(n):
        col = a[:, j:j + 1]
        row = a[j:j + 1, :]
        root = jnp.sqrt(a[j:j + 1, j:j + 1])
        lcol = jnp.where(colv >= j, col / root, 0.0)
        lrow = jnp.where(cols[:1] >= j, row / root, 0.0)
        a = a - lcol * lrow
        lcols.append(lcol)
        diags.append(root)
    c = jnp.zeros((n, n), jnp.float32)
    for i in reversed(range(n)):
        part = jnp.sum(jnp.where(colv > i, lcols[i], 0.0) * c, axis=0, keepdims=True)
        r = jnp.where(cols[:1] == i, 1.0, 0.0) - part
        c = jnp.where(rows == i, r / diags[i], c)
    c_ref[...] = c


def upper_inverse(gram):
    sym = 0.5 * (gram + gram.T)
    return pl.pallas_call(
        _upper_inverse_kernel,
        out_shape=jax.ShapeDtypeStruct(gram.shape, jnp.float32),
        in_specs=[pl.BlockSpec(memory_space=pltpu.VMEM)],
        out_specs=pl.BlockSpec(memory_space=pltpu.VMEM),
    )(sym)


def local(potential, start_basis):
    mine = start_basis.shape[0]
    rows = start_basis.shape[2] // 2
    v = lax.axis_index("vec")
    n = lax.axis_size(AXES)
    groups = radix_groups(n)
    scale = 1.0 / (
        start_basis.shape[1] * start_basis.shape[2] * start_basis.shape[3] * lax.axis_size("space")
    )

    def in_order(a, b, axis):
        return jnp.where(v == 0, jnp.concatenate([a, b], axis), jnp.concatenate([b, a], axis))

    ext = jnp.concatenate([start_basis[:, :, -1:], start_basis, start_basis[:, :, :1]], axis=2)
    keep = lax.dynamic_slice_in_dim(ext, v * rows, rows + 2, 2)
    give = lax.dynamic_slice_in_dim(ext, (1 - v) * rows, rows + 2, 2)
    got = swap_vec(give)
    same_up = [(i, (i + 2) % n) for i in range(n)]
    same_down = [(j, i) for i, j in same_up]
    cross_up = [(i, ((i // 2 + 1) * 2 + 1 - i % 2) % n) for i in range(n)]
    cross_down = [(j, i) for i, j in cross_up]
    keep_rows = keep[:, :, 1:-1]
    give_rows = give[:, :, 1:-1]
    before = in_order(lax.ppermute(keep_rows, AXES, same_up), lax.ppermute(give_rows, AXES, cross_up), 0)
    after = in_order(lax.ppermute(keep_rows, AXES, same_down), lax.ppermute(give_rows, AXES, cross_down), 0)
    whole_ext = in_order(keep, got, 0)
    whole = whole_ext[:, :, 1:-1]
    ends = jnp.concatenate([whole_ext[:, :, :1], whole_ext[:, :, -1:]], axis=2)

    pot = lax.dynamic_slice_in_dim(potential, v * rows, rows, 1)
    shifted = jnp.where(pot >= SIGMA, pot - SIGMA + 6.0, pot - SIGMA - 6.0)

    h_whole = stencil(whole, (before, after, ends), pot)
    nb = whole.shape[0]
    fields = jnp.concatenate([whole, h_whole, whole / shifted, h_whole / shifted], 0)
    first = allsum(local_inner(fields[: 2 * nb], fields, scale), groups)
    gram = first[:nb, :nb]
    g_sh = first[:nb, nb:2 * nb]
    u_ss = first[:nb, 2 * nb:3 * nb]
    u_sh = first[:nb, 3 * nb:]
    u_hs = first[nb:, 2 * nb:3 * nb]
    u_hh = first[nb:, 3 * nb:]
    cmat = upper_inverse(gram)
    ct = cmat.T
    rayleigh = mm(ct, mm(g_sh, cmat))
    b_b = mm(ct, mm(gram, cmat))
    ab_b = mm(ct, mm(g_sh.T, cmat)) - SIGMA * b_b

    cr = mm(cmat, rayleigh)
    s_rd = mm(u_sh, cmat) - mm(u_ss, cr)
    h_rd = mm(u_hh, cmat) - mm(u_hs, cr)
    coeff = -mm(ct, s_rd)
    ab_c = -mm(ct, h_rd - SIGMA * s_rd)
    back = ab_c - mm(ab_b, coeff)
    zero = jnp.zeros_like(cmat)
    weights = jnp.concatenate(
        [
            jnp.concatenate([cmat, -SIGMA * cmat, -cr, mm(cmat, coeff)], 1),
            jnp.concatenate([zero, cmat, cmat, zero], 1),
        ],
        0,
    )
    parts = combine(weights, jnp.concatenate([whole, h_whole], 0))
    both = parts[: 2 * nb]
    basis, a_basis, resid = parts[:nb], parts[nb:2 * nb], parts[2 * nb:3 * nb]
    correction = -resid / shifted
    proj = correction - parts[3 * nb:]
    pieces = halo(proj)

    moved = stencil(proj, pieces, pot) - SIGMA * proj
    correction = correction + (-resid - (moved - combine(back, basis))) / shifted

    for sweep in range(2, NSWEEP):
        pieces = halo(correction)
        red = allsum(local_inner(both, correction, scale), groups)
        coeff = red[:nb]
        back = red[nb:] - mm(ab_b, coeff)
        moved = stencil(correction, pieces, pot) - SIGMA * correction - combine(coeff, a_basis)
        correction = correction + (-resid - (moved - combine(back, basis))) / shifted

    red = allsum(
        jnp.concatenate([local_inner(basis, correction, scale), local_inner(correction, correction, scale)], 0),
        groups,
    )
    proj_two = red[:nb]
    gram_two = red[nb:] - 2.0 * mm(proj_two.T, proj_two) + mm(proj_two.T, mm(b_b, proj_two))
    fresh = correction - combine(proj_two, basis)
    new_all = combine(upper_inverse(gram_two), fresh)

    own = lax.dynamic_slice_in_dim(new_all, v * mine, mine, 0)
    out = lax.dynamic_slice_in_dim(new_all, (1 - v) * mine, mine, 0)
    new_basis = in_order(own, swap_vec(out), 2)
    return (new_basis, rayleigh)


def solution(mesh):
    in_specs = (P("space", None, None), P("vec", "space", None, None))
    out_specs = (P("vec", "space", None, None), P())
    return jax.shard_map(local, mesh=mesh, in_specs=in_specs, out_specs=out_specs, check_vma=False)
```

```python
import jax
import jax.numpy as jnp
from jax import lax
from jax.sharding import PartitionSpec as P

NSWEEP = 3


SIGMA = 0.5
PREC = lax.Precision.HIGHEST
FIELD_PREC = lax.Precision.HIGH
AXES = ("space", "vec")


def allsum(x, groups):
    n = lax.axis_size(AXES)
    for group in groups:
        vals = {0: x}
        for m in range(1, 1 << len(group)):
            mask = sum(1 << b for t, b in enumerate(group) if (m >> t) & 1)
            vals[m] = lax.ppermute(x, AXES, [(i, i ^ mask) for i in range(n)])
        for t in range(len(group)):
            vals = {m: vals[m] + vals[m | (1 << t)] for m in vals if not (m >> t) & 1}
        x = vals[0]
    return x


def radix_groups(n):
    bits = n.bit_length() - 1
    return [[0]] + [list(range(i, min(i + 2, bits))) for i in range(1, bits, 2)]


def local_inner(left, right, scale):
    return jnp.einsum("kzyx,jzyx->kj", left, right, precision=FIELD_PREC) * scale


def combine(coeff, vectors):
    return jnp.einsum("kj,kzyx->jzyx", coeff, vectors, precision=FIELD_PREC)


def mm(a, b):
    return jnp.matmul(a, b, precision=PREC)


def swap_vec(value):
    return lax.ppermute(value, "vec", [(0, 1), (1, 0)])


def halo(value):
    peers = lax.axis_size("space")
    up = [(i, (i + 1) % peers) for i in range(peers)]
    down = [(j, i) for i, j in up]
    rows = value.shape[2]
    edge = jnp.concatenate([value[:, :, rows - 1:], value[:, :, :1]], axis=2)
    before = lax.ppermute(value, "space", up)
    after = lax.ppermute(value, "space", down)
    ends = swap_vec(edge)
    return before, after, ends


def stencil(value, pieces, potential):
    before, after, ends = pieces
    ext = jnp.concatenate([ends[:, :, :1], value, ends[:, :, 1:]], axis=2)
    beside = before + after
    beside = beside + ext[:, :, :-2] + ext[:, :, 2:]
    beside = beside + jnp.roll(value, 1, 3) + jnp.roll(value, -1, 3)
    return potential * value - beside


def inverse_factor(gram):
    lower = jnp.linalg.cholesky(gram)
    return jax.scipy.linalg.solve_triangular(
        lower, jnp.eye(gram.shape[0], dtype=jnp.float32), lower=True
    )


def local(potential, start_basis):
    mine = start_basis.shape[0]
    rows = start_basis.shape[2] // 2
    v = lax.axis_index("vec")
    n = lax.axis_size(AXES)
    groups = radix_groups(n)
    scale = 1.0 / (
        start_basis.shape[1] * start_basis.shape[2] * start_basis.shape[3] * lax.axis_size("space")
    )

    def in_order(a, b, axis):
        return jnp.where(v == 0, jnp.concatenate([a, b], axis), jnp.concatenate([b, a], axis))

    ext = jnp.concatenate([start_basis[:, :, -1:], start_basis, start_basis[:, :, :1]], axis=2)
    keep = lax.dynamic_slice_in_dim(ext, v * rows, rows + 2, 2)
    give = lax.dynamic_slice_in_dim(ext, (1 - v) * rows, rows + 2, 2)
    got = swap_vec(give)
    same_up = [(i, (i + 2) % n) for i in range(n)]
    same_down = [(j, i) for i, j in same_up]
    cross_up = [(i, ((i // 2 + 1) * 2 + 1 - i % 2) % n) for i in range(n)]
    cross_down = [(j, i) for i, j in cross_up]
    keep_rows = keep[:, :, 1:-1]
    give_rows = give[:, :, 1:-1]
    before = in_order(lax.ppermute(keep_rows, AXES, same_up), lax.ppermute(give_rows, AXES, cross_up), 0)
    after = in_order(lax.ppermute(keep_rows, AXES, same_down), lax.ppermute(give_rows, AXES, cross_down), 0)
    whole_ext = in_order(keep, got, 0)
    whole = whole_ext[:, :, 1:-1]
    ends = jnp.concatenate([whole_ext[:, :, :1], whole_ext[:, :, -1:]], axis=2)

    pot = lax.dynamic_slice_in_dim(potential, v * rows, rows, 1)
    shifted = jnp.where(pot >= SIGMA, pot - SIGMA + 6.0, pot - SIGMA - 6.0)

    h_whole = stencil(whole, (before, after, ends), pot)
    nb = whole.shape[0]
    fields = jnp.concatenate([whole, h_whole, whole / shifted, h_whole / shifted], 0)
    first = allsum(local_inner(fields[: 2 * nb], fields, scale), groups)
    gram = first[:nb, :nb]
    g_sh = first[:nb, nb:2 * nb]
    u_ss = first[:nb, 2 * nb:3 * nb]
    u_sh = first[:nb, 3 * nb:]
    u_hs = first[nb:, 2 * nb:3 * nb]
    u_hh = first[nb:, 3 * nb:]
    cmat = inverse_factor(gram).T
    ct = cmat.T
    rayleigh = mm(ct, mm(g_sh, cmat))
    b_b = mm(ct, mm(gram, cmat))
    ab_b = mm(ct, mm(g_sh.T, cmat)) - SIGMA * b_b

    cr = mm(cmat, rayleigh)
    s_rd = mm(u_sh, cmat) - mm(u_ss, cr)
    h_rd = mm(u_hh, cmat) - mm(u_hs, cr)
    coeff = -mm(ct, s_rd)
    ab_c = -mm(ct, h_rd - SIGMA * s_rd)
    back = ab_c - mm(ab_b, coeff)
    zero = jnp.zeros_like(cmat)
    weights = jnp.concatenate(
        [
            jnp.concatenate([cmat, -SIGMA * cmat, -cr, mm(cmat, coeff)], 1),
            jnp.concatenate([zero, cmat, cmat, zero], 1),
        ],
        0,
    )
    parts = combine(weights, jnp.concatenate([whole, h_whole], 0))
    both = parts[: 2 * nb]
    basis, a_basis, resid = parts[:nb], parts[nb:2 * nb], parts[2 * nb:3 * nb]
    correction = -resid / shifted
    proj = correction - parts[3 * nb:]
    pieces = halo(proj)

    moved = stencil(proj, pieces, pot) - SIGMA * proj
    correction = correction + (-resid - (moved - combine(back, basis))) / shifted

    for sweep in range(2, NSWEEP):
        pieces = halo(correction)
        red = allsum(local_inner(both, correction, scale), groups)
        coeff = red[:nb]
        back = red[nb:] - mm(ab_b, coeff)
        moved = stencil(correction, pieces, pot) - SIGMA * correction - combine(coeff, a_basis)
        correction = correction + (-resid - (moved - combine(back, basis))) / shifted

    red = allsum(
        jnp.concatenate([local_inner(basis, correction, scale), local_inner(correction, correction, scale)], 0),
        groups,
    )
    proj_two = red[:nb]
    gram_two = red[nb:] - 2.0 * mm(proj_two.T, proj_two) + mm(proj_two.T, mm(b_b, proj_two))
    fresh = correction - combine(proj_two, basis)
    new_all = combine(inverse_factor(gram_two).T, fresh)

    new_basis = lax.all_to_all(new_all, "vec", 0, 2, tiled=True)
    return (new_basis, rayleigh)


def solution(mesh):
    in_specs = (P("space", None, None), P("vec", "space", None, None))
    out_specs = (P("vec", "space", None, None), P())
    return jax.shard_map(local, mesh=mesh, in_specs=in_specs, out_specs=out_specs, check_vma=False)
```

```python
import jax
import jax.numpy as jnp
from jax import lax
from jax.sharding import PartitionSpec as P

NSWEEP = 3


SIGMA = 0.5
PREC = lax.Precision.HIGHEST
FIELD_PREC = lax.Precision.HIGH
AXES = ("space", "vec")


def allsum(x, groups):
    n = lax.axis_size(AXES)
    for group in groups:
        vals = {0: x}
        for m in range(1, 1 << len(group)):
            mask = sum(1 << b for t, b in enumerate(group) if (m >> t) & 1)
            vals[m] = lax.ppermute(x, AXES, [(i, i ^ mask) for i in range(n)])
        for t in range(len(group)):
            vals = {m: vals[m] + vals[m | (1 << t)] for m in vals if not (m >> t) & 1}
        x = vals[0]
    return x


def radix_groups(n):
    bits = n.bit_length() - 1
    return [[0]] + [list(range(i, min(i + 2, bits))) for i in range(1, bits, 2)]


def local_inner(left, right, scale):
    return jnp.einsum("kzyx,jzyx->kj", left, right, precision=FIELD_PREC) * scale


def combine(coeff, vectors):
    return jnp.einsum("kj,kzyx->jzyx", coeff, vectors, precision=FIELD_PREC)


def mm(a, b):
    return jnp.matmul(a, b, precision=PREC)


def swap_vec(value):
    return lax.ppermute(value, "vec", [(0, 1), (1, 0)])


def halo(value):
    peers = lax.axis_size("space")
    up = [(i, (i + 1) % peers) for i in range(peers)]
    down = [(j, i) for i, j in up]
    rows = value.shape[2]
    edge = jnp.concatenate([value[:, :, rows - 1:], value[:, :, :1]], axis=2)
    before = lax.ppermute(value, "space", up)
    after = lax.ppermute(value, "space", down)
    ends = swap_vec(edge)
    return before, after, ends


def stencil(value, pieces, potential):
    before, after, ends = pieces
    ext = jnp.concatenate([ends[:, :, :1], value, ends[:, :, 1:]], axis=2)
    beside = before + after
    beside = beside + ext[:, :, :-2] + ext[:, :, 2:]
    beside = beside + jnp.roll(value, 1, 3) + jnp.roll(value, -1, 3)
    return potential * value - beside


def inverse_factor(gram):
    lower = jnp.linalg.cholesky(gram)
    return jax.scipy.linalg.solve_triangular(
        lower, jnp.eye(gram.shape[0], dtype=jnp.float32), lower=True
    )


def local(potential, start_basis):
    mine = start_basis.shape[0]
    rows = start_basis.shape[2] // 2
    v = lax.axis_index("vec")
    n = lax.axis_size(AXES)
    groups = radix_groups(n)
    scale = 1.0 / (
        start_basis.shape[1] * start_basis.shape[2] * start_basis.shape[3] * lax.axis_size("space")
    )

    def in_order(a, b, axis):
        return jnp.where(v == 0, jnp.concatenate([a, b], axis), jnp.concatenate([b, a], axis))

    keep_rows = lax.dynamic_slice_in_dim(start_basis, v * rows, rows, 2)
    give_rows = lax.dynamic_slice_in_dim(start_basis, (1 - v) * rows, rows, 2)
    got = swap_vec(give_rows)
    got_ends = swap_vec(jnp.concatenate([keep_rows[:, :, rows - 1:], keep_rows[:, :, :1]], axis=2))
    own_ends = jnp.concatenate(
        [
            lax.dynamic_slice_in_dim(start_basis, (v * rows - 1) % (2 * rows), 1, 2),
            lax.dynamic_slice_in_dim(start_basis, (v * rows + rows) % (2 * rows), 1, 2),
        ],
        axis=2,
    )
    same_up = [(i, (i + 2) % n) for i in range(n)]
    same_down = [(j, i) for i, j in same_up]
    cross_up = [(i, ((i // 2 + 1) * 2 + 1 - i % 2) % n) for i in range(n)]
    cross_down = [(j, i) for i, j in cross_up]
    before = in_order(lax.ppermute(keep_rows, AXES, same_up), lax.ppermute(give_rows, AXES, cross_up), 0)
    after = in_order(lax.ppermute(keep_rows, AXES, same_down), lax.ppermute(give_rows, AXES, cross_down), 0)
    whole = in_order(keep_rows, got, 0)
    ends = in_order(own_ends, got_ends, 0)

    pot = lax.dynamic_slice_in_dim(potential, v * rows, rows, 1)
    shifted = jnp.where(pot >= SIGMA, pot - SIGMA + 6.0, pot - SIGMA - 6.0)

    h_whole = stencil(whole, (before, after, ends), pot)
    nb = whole.shape[0]
    fields = jnp.concatenate([whole, h_whole], 0)
    first = allsum(
        jnp.concatenate(
            [local_inner(fields, fields, scale), local_inner(fields, fields / shifted, scale)], 1
        ),
        groups,
    )
    gram = first[:nb, :nb]
    g_sh = first[:nb, nb:2 * nb]
    u_ss = first[:nb, 2 * nb:3 * nb]
    u_sh = first[:nb, 3 * nb:]
    u_hs = first[nb:, 2 * nb:3 * nb]
    u_hh = first[nb:, 3 * nb:]
    cmat = inverse_factor(gram).T
    ct = cmat.T
    rayleigh = mm(ct, mm(g_sh, cmat))
    b_b = mm(ct, mm(gram, cmat))
    ab_b = mm(ct, mm(g_sh.T, cmat)) - SIGMA * b_b

    cr = mm(cmat, rayleigh)
    s_rd = mm(u_sh, cmat) - mm(u_ss, cr)
    h_rd = mm(u_hh, cmat) - mm(u_hs, cr)
    coeff = -mm(ct, s_rd)
    ab_c = -mm(ct, h_rd - SIGMA * s_rd)
    back = ab_c - mm(ab_b, coeff)
    zero = jnp.zeros_like(cmat)
    weights = jnp.concatenate(
        [
            jnp.concatenate([cmat, -SIGMA * cmat, -cr, mm(cmat, coeff)], 1),
            jnp.concatenate([zero, cmat, cmat, zero], 1),
        ],
        0,
    )
    parts = combine(weights, jnp.concatenate([whole, h_whole], 0))
    both = parts[: 2 * nb]
    basis, a_basis, resid = parts[:nb], parts[nb:2 * nb], parts[2 * nb:3 * nb]
    correction = -resid / shifted
    proj = correction - parts[3 * nb:]
    pieces = halo(proj)

    moved = stencil(proj, pieces, pot) - SIGMA * proj
    correction = correction + (-resid - (moved - combine(back, basis))) / shifted

    for sweep in range(2, NSWEEP):
        pieces = halo(correction)
        red = allsum(local_inner(both, correction, scale), groups)
        coeff = red[:nb]
        back = red[nb:] - mm(ab_b, coeff)
        moved = stencil(correction, pieces, pot) - SIGMA * correction - combine(coeff, a_basis)
        correction = correction + (-resid - (moved - combine(back, basis))) / shifted

    red = allsum(
        jnp.concatenate([local_inner(basis, correction, scale), local_inner(correction, correction, scale)], 0),
        groups,
    )
    proj_two = red[:nb]
    gram_two = red[nb:] - 2.0 * mm(proj_two.T, proj_two) + mm(proj_two.T, mm(b_b, proj_two))
    fresh = correction - combine(proj_two, basis)
    new_all = combine(inverse_factor(gram_two).T, fresh)

    own = lax.dynamic_slice_in_dim(new_all, v * mine, mine, 0)
    out = lax.dynamic_slice_in_dim(new_all, (1 - v) * mine, mine, 0)
    new_basis = in_order(own, swap_vec(out), 2)
    return (new_basis, rayleigh)


def solution(mesh):
    in_specs = (P("space", None, None), P("vec", "space", None, None))
    out_specs = (P("vec", "space", None, None), P())
    return jax.shard_map(local, mesh=mesh, in_specs=in_specs, out_specs=out_specs, check_vma=False)
```

```python
import jax
import jax.numpy as jnp
from jax import lax
from jax.sharding import PartitionSpec as P

NSWEEP = 3


SIGMA = 0.5
PREC = lax.Precision.HIGHEST
FIELD_PREC = lax.Precision.HIGH
AXES = ("space", "vec")


def allsum(x, groups):
    n = lax.axis_size(AXES)
    for group in groups:
        vals = {0: x}
        for m in range(1, 1 << len(group)):
            mask = sum(1 << b for t, b in enumerate(group) if (m >> t) & 1)
            vals[m] = lax.ppermute(x, AXES, [(i, i ^ mask) for i in range(n)])
        for t in range(len(group)):
            vals = {m: vals[m] + vals[m | (1 << t)] for m in vals if not (m >> t) & 1}
        x = vals[0]
    return x


def radix_groups(n):
    bits = n.bit_length() - 1
    return [[0]] + [list(range(i, min(i + 2, bits))) for i in range(1, bits, 2)]


def local_inner(left, right, scale):
    return jnp.einsum("kzyx,jzyx->kj", left, right, precision=PREC) * scale


def combine(coeff, vectors):
    return jnp.einsum("kj,kzyx->jzyx", coeff, vectors, precision=FIELD_PREC)


def mm(a, b):
    return jnp.matmul(a, b, precision=PREC)


def swap_vec(value):
    return lax.ppermute(value, "vec", [(0, 1), (1, 0)])


def halo(value):
    peers = lax.axis_size("space")
    up = [(i, (i + 1) % peers) for i in range(peers)]
    down = [(j, i) for i, j in up]
    rows = value.shape[2]
    edge = jnp.concatenate([value[:, :, rows - 1:], value[:, :, :1]], axis=2)
    before = lax.ppermute(value, "space", up)
    after = lax.ppermute(value, "space", down)
    ends = swap_vec(edge)
    return before, after, ends


def stencil(value, pieces, potential):
    before, after, ends = pieces
    ext = jnp.concatenate([ends[:, :, :1], value, ends[:, :, 1:]], axis=2)
    beside = before + after
    beside = beside + ext[:, :, :-2] + ext[:, :, 2:]
    beside = beside + jnp.roll(value, 1, 3) + jnp.roll(value, -1, 3)
    return potential * value - beside


def inverse_factor(gram):
    lower = jnp.linalg.cholesky(gram)
    return jax.scipy.linalg.solve_triangular(
        lower, jnp.eye(gram.shape[0], dtype=jnp.float32), lower=True
    )


def local(potential, start_basis):
    mine = start_basis.shape[0]
    rows = start_basis.shape[2] // 2
    v = lax.axis_index("vec")
    n = lax.axis_size(AXES)
    groups = radix_groups(n)
    scale = 1.0 / (
        start_basis.shape[1] * start_basis.shape[2] * start_basis.shape[3] * lax.axis_size("space")
    )

    def in_order(a, b, axis):
        return jnp.where(v == 0, jnp.concatenate([a, b], axis), jnp.concatenate([b, a], axis))

    ext = jnp.concatenate([start_basis[:, :, -1:], start_basis, start_basis[:, :, :1]], axis=2)
    keep = lax.dynamic_slice_in_dim(ext, v * rows, rows + 2, 2)
    give = lax.dynamic_slice_in_dim(ext, (1 - v) * rows, rows + 2, 2)
    got = swap_vec(give)
    same_up = [(i, (i + 2) % n) for i in range(n)]
    same_down = [(j, i) for i, j in same_up]
    cross_up = [(i, ((i // 2 + 1) * 2 + 1 - i % 2) % n) for i in range(n)]
    cross_down = [(j, i) for i, j in cross_up]
    keep_rows = keep[:, :, 1:-1]
    give_rows = give[:, :, 1:-1]
    before = in_order(lax.ppermute(keep_rows, AXES, same_up), lax.ppermute(give_rows, AXES, cross_up), 0)
    after = in_order(lax.ppermute(keep_rows, AXES, same_down), lax.ppermute(give_rows, AXES, cross_down), 0)
    whole_ext = in_order(keep, got, 0)
    whole = whole_ext[:, :, 1:-1]
    ends = jnp.concatenate([whole_ext[:, :, :1], whole_ext[:, :, -1:]], axis=2)

    pot = lax.dynamic_slice_in_dim(potential, v * rows, rows, 1)
    shifted = jnp.where(pot >= SIGMA, pot - SIGMA + 6.0, pot - SIGMA - 6.0)

    h_whole = stencil(whole, (before, after, ends), pot)
    nb = whole.shape[0]
    fields = jnp.concatenate([whole, h_whole, whole / shifted, h_whole / shifted], 0)
    first = allsum(local_inner(fields[: 2 * nb], fields, scale), groups)
    gram = first[:nb, :nb]
    g_sh = first[:nb, nb:2 * nb]
    u_ss = first[:nb, 2 * nb:3 * nb]
    u_sh = first[:nb, 3 * nb:]
    u_hs = first[nb:, 2 * nb:3 * nb]
    u_hh = first[nb:, 3 * nb:]
    cmat = inverse_factor(gram).T
    ct = cmat.T
    rayleigh = mm(ct, mm(g_sh, cmat))
    b_b = mm(ct, mm(gram, cmat))
    ab_b = mm(ct, mm(g_sh.T, cmat)) - SIGMA * b_b

    cr = mm(cmat, rayleigh)
    s_rd = mm(u_sh, cmat) - mm(u_ss, cr)
    h_rd = mm(u_hh, cmat) - mm(u_hs, cr)
    coeff = -mm(ct, s_rd)
    ab_c = -mm(ct, h_rd - SIGMA * s_rd)
    back = ab_c - mm(ab_b, coeff)
    zero = jnp.zeros_like(cmat)
    weights = jnp.concatenate(
        [
            jnp.concatenate([cmat, -SIGMA * cmat, -cr, mm(cmat, coeff)], 1),
            jnp.concatenate([zero, cmat, cmat, zero], 1),
        ],
        0,
    )
    parts = combine(weights, jnp.concatenate([whole, h_whole], 0))
    both = parts[: 2 * nb]
    basis, a_basis, resid = parts[:nb], parts[nb:2 * nb], parts[2 * nb:3 * nb]
    correction = -resid / shifted
    proj = correction - parts[3 * nb:]
    pieces = halo(proj)

    moved = stencil(proj, pieces, pot) - SIGMA * proj
    correction = correction + (-resid - (moved - combine(back, basis))) / shifted

    for sweep in range(2, NSWEEP):
        pieces = halo(correction)
        red = allsum(local_inner(both, correction, scale), groups)
        coeff = red[:nb]
        back = red[nb:] - mm(ab_b, coeff)
        moved = stencil(correction, pieces, pot) - SIGMA * correction - combine(coeff, a_basis)
        correction = correction + (-resid - (moved - combine(back, basis))) / shifted

    red = allsum(
        jnp.concatenate([local_inner(basis, correction, scale), local_inner(correction, correction, scale)], 0),
        groups,
    )
    proj_two = red[:nb]
    gram_two = red[nb:] - 2.0 * mm(proj_two.T, proj_two) + mm(proj_two.T, mm(b_b, proj_two))
    fresh = correction - combine(proj_two, basis)
    new_all = combine(inverse_factor(gram_two).T, fresh)

    own = lax.dynamic_slice_in_dim(new_all, v * mine, mine, 0)
    out = lax.dynamic_slice_in_dim(new_all, (1 - v) * mine, mine, 0)
    new_basis = in_order(own, swap_vec(out), 2)
    return (new_basis, rayleigh)


def solution(mesh):
    in_specs = (P("space", None, None), P("vec", "space", None, None))
    out_specs = (P("vec", "space", None, None), P())
    return jax.shard_map(local, mesh=mesh, in_specs=in_specs, out_specs=out_specs, check_vma=False)
```

```python
import jax
import jax.numpy as jnp
from jax import lax
from jax.sharding import PartitionSpec as P

NSWEEP = 3


SIGMA = 0.5
PREC = lax.Precision.HIGHEST
FIELD_PREC = lax.Precision.HIGH
AXES = ("space", "vec")


def allsum(x, groups):
    n = lax.axis_size(AXES)
    for group in groups:
        vals = {0: x}
        for m in range(1, 1 << len(group)):
            mask = sum(1 << b for t, b in enumerate(group) if (m >> t) & 1)
            vals[m] = lax.ppermute(x, AXES, [(i, i ^ mask) for i in range(n)])
        for t in range(len(group)):
            vals = {m: vals[m] + vals[m | (1 << t)] for m in vals if not (m >> t) & 1}
        x = vals[0]
    return x


def radix_groups(n):
    bits = n.bit_length() - 1
    return [[0]] + [list(range(i, min(i + 2, bits))) for i in range(1, bits, 2)]


def local_inner(left, right, scale):
    return jnp.einsum("kzyx,jzyx->kj", left, right, precision=FIELD_PREC) * scale


def combine(coeff, vectors):
    return jnp.einsum("kj,kzyx->jzyx", coeff, vectors, precision=PREC)


def mm(a, b):
    return jnp.matmul(a, b, precision=PREC)


def swap_vec(value):
    return lax.ppermute(value, "vec", [(0, 1), (1, 0)])


def halo(value):
    peers = lax.axis_size("space")
    up = [(i, (i + 1) % peers) for i in range(peers)]
    down = [(j, i) for i, j in up]
    rows = value.shape[2]
    edge = jnp.concatenate([value[:, :, rows - 1:], value[:, :, :1]], axis=2)
    before = lax.ppermute(value, "space", up)
    after = lax.ppermute(value, "space", down)
    ends = swap_vec(edge)
    return before, after, ends


def stencil(value, pieces, potential):
    before, after, ends = pieces
    ext = jnp.concatenate([ends[:, :, :1], value, ends[:, :, 1:]], axis=2)
    beside = before + after
    beside = beside + ext[:, :, :-2] + ext[:, :, 2:]
    beside = beside + jnp.roll(value, 1, 3) + jnp.roll(value, -1, 3)
    return potential * value - beside


def inverse_factor(gram):
    lower = jnp.linalg.cholesky(gram)
    return jax.scipy.linalg.solve_triangular(
        lower, jnp.eye(gram.shape[0], dtype=jnp.float32), lower=True
    )


def local(potential, start_basis):
    mine = start_basis.shape[0]
    rows = start_basis.shape[2] // 2
    v = lax.axis_index("vec")
    n = lax.axis_size(AXES)
    groups = radix_groups(n)
    scale = 1.0 / (
        start_basis.shape[1] * start_basis.shape[2] * start_basis.shape[3] * lax.axis_size("space")
    )

    def in_order(a, b, axis):
        return jnp.where(v == 0, jnp.concatenate([a, b], axis), jnp.concatenate([b, a], axis))

    ext = jnp.concatenate([start_basis[:, :, -1:], start_basis, start_basis[:, :, :1]], axis=2)
    keep = lax.dynamic_slice_in_dim(ext, v * rows, rows + 2, 2)
    give = lax.dynamic_slice_in_dim(ext, (1 - v) * rows, rows + 2, 2)
    got = swap_vec(give)
    same_up = [(i, (i + 2) % n) for i in range(n)]
    same_down = [(j, i) for i, j in same_up]
    cross_up = [(i, ((i // 2 + 1) * 2 + 1 - i % 2) % n) for i in range(n)]
    cross_down = [(j, i) for i, j in cross_up]
    keep_rows = keep[:, :, 1:-1]
    give_rows = give[:, :, 1:-1]
    before = in_order(lax.ppermute(keep_rows, AXES, same_up), lax.ppermute(give_rows, AXES, cross_up), 0)
    after = in_order(lax.ppermute(keep_rows, AXES, same_down), lax.ppermute(give_rows, AXES, cross_down), 0)
    whole_ext = in_order(keep, got, 0)
    whole = whole_ext[:, :, 1:-1]
    ends = jnp.concatenate([whole_ext[:, :, :1], whole_ext[:, :, -1:]], axis=2)

    pot = lax.dynamic_slice_in_dim(potential, v * rows, rows, 1)
    shifted = jnp.where(pot >= SIGMA, pot - SIGMA + 6.0, pot - SIGMA - 6.0)

    h_whole = stencil(whole, (before, after, ends), pot)
    nb = whole.shape[0]
    fields = jnp.concatenate([whole, h_whole, whole / shifted, h_whole / shifted], 0)
    first = allsum(local_inner(fields[: 2 * nb], fields, scale), groups)
    gram = first[:nb, :nb]
    g_sh = first[:nb, nb:2 * nb]
    u_ss = first[:nb, 2 * nb:3 * nb]
    u_sh = first[:nb, 3 * nb:]
    u_hs = first[nb:, 2 * nb:3 * nb]
    u_hh = first[nb:, 3 * nb:]
    cmat = inverse_factor(gram).T
    ct = cmat.T
    rayleigh = mm(ct, mm(g_sh, cmat))
    b_b = mm(ct, mm(gram, cmat))
    ab_b = mm(ct, mm(g_sh.T, cmat)) - SIGMA * b_b

    cr = mm(cmat, rayleigh)
    s_rd = mm(u_sh, cmat) - mm(u_ss, cr)
    h_rd = mm(u_hh, cmat) - mm(u_hs, cr)
    coeff = -mm(ct, s_rd)
    ab_c = -mm(ct, h_rd - SIGMA * s_rd)
    back = ab_c - mm(ab_b, coeff)
    zero = jnp.zeros_like(cmat)
    weights = jnp.concatenate(
        [
            jnp.concatenate([cmat, -SIGMA * cmat, -cr, mm(cmat, coeff)], 1),
            jnp.concatenate([zero, cmat, cmat, zero], 1),
        ],
        0,
    )
    parts = combine(weights, jnp.concatenate([whole, h_whole], 0))
    both = parts[: 2 * nb]
    basis, a_basis, resid = parts[:nb], parts[nb:2 * nb], parts[2 * nb:3 * nb]
    correction = -resid / shifted
    proj = correction - parts[3 * nb:]
    pieces = halo(proj)

    moved = stencil(proj, pieces, pot) - SIGMA * proj
    correction = correction + (-resid - (moved - combine(back, basis))) / shifted

    for sweep in range(2, NSWEEP):
        pieces = halo(correction)
        red = allsum(local_inner(both, correction, scale), groups)
        coeff = red[:nb]
        back = red[nb:] - mm(ab_b, coeff)
        moved = stencil(correction, pieces, pot) - SIGMA * correction - combine(coeff, a_basis)
        correction = correction + (-resid - (moved - combine(back, basis))) / shifted

    red = allsum(
        jnp.concatenate([local_inner(basis, correction, scale), local_inner(correction, correction, scale)], 0),
        groups,
    )
    proj_two = red[:nb]
    gram_two = red[nb:] - 2.0 * mm(proj_two.T, proj_two) + mm(proj_two.T, mm(b_b, proj_two))
    fresh = correction - combine(proj_two, basis)
    new_all = combine(inverse_factor(gram_two).T, fresh)

    own = lax.dynamic_slice_in_dim(new_all, v * mine, mine, 0)
    out = lax.dynamic_slice_in_dim(new_all, (1 - v) * mine, mine, 0)
    new_basis = in_order(own, swap_vec(out), 2)
    return (new_basis, rayleigh)


def solution(mesh):
    in_specs = (P("space", None, None), P("vec", "space", None, None))
    out_specs = (P("vec", "space", None, None), P())
    return jax.shard_map(local, mesh=mesh, in_specs=in_specs, out_specs=out_specs, check_vma=False)
```

```python
import jax
import jax.numpy as jnp
from jax import lax
from jax.sharding import PartitionSpec as P

NSWEEP = 3


SIGMA = 0.5
PREC = lax.Precision.HIGHEST
FIELD_PREC = lax.Precision.HIGH
AXES = ("space", "vec")


def allsum(x, groups):
    n = lax.axis_size(AXES)
    for group in groups:
        vals = {0: x}
        for m in range(1, 1 << len(group)):
            mask = sum(1 << b for t, b in enumerate(group) if (m >> t) & 1)
            vals[m] = lax.ppermute(x, AXES, [(i, i ^ mask) for i in range(n)])
        for t in range(len(group)):
            vals = {m: vals[m] + vals[m | (1 << t)] for m in vals if not (m >> t) & 1}
        x = vals[0]
    return x


def radix_groups(n):
    bits = n.bit_length() - 1
    return [[0]] + [list(range(i, min(i + 2, bits))) for i in range(1, bits, 2)]


def local_inner(left, right, scale):
    return jnp.einsum("kzyx,jzyx->kj", left, right, precision=FIELD_PREC) * scale


def combine(coeff, vectors, precision=FIELD_PREC):
    return jnp.einsum("kj,kzyx->jzyx", coeff, vectors, precision=precision)


def mm(a, b):
    return jnp.matmul(a, b, precision=PREC)


def swap_vec(value):
    return lax.ppermute(value, "vec", [(0, 1), (1, 0)])


def halo(value):
    peers = lax.axis_size("space")
    up = [(i, (i + 1) % peers) for i in range(peers)]
    down = [(j, i) for i, j in up]
    rows = value.shape[2]
    edge = jnp.concatenate([value[:, :, rows - 1:], value[:, :, :1]], axis=2)
    before = lax.ppermute(value, "space", up)
    after = lax.ppermute(value, "space", down)
    ends = swap_vec(edge)
    return before, after, ends


def stencil(value, pieces, potential):
    before, after, ends = pieces
    ext = jnp.concatenate([ends[:, :, :1], value, ends[:, :, 1:]], axis=2)
    beside = before + after
    beside = beside + ext[:, :, :-2] + ext[:, :, 2:]
    beside = beside + jnp.roll(value, 1, 3) + jnp.roll(value, -1, 3)
    return potential * value - beside


def inverse_factor(gram):
    lower = jnp.linalg.cholesky(gram)
    return jax.scipy.linalg.solve_triangular(
        lower, jnp.eye(gram.shape[0], dtype=jnp.float32), lower=True
    )


def local(potential, start_basis):
    mine = start_basis.shape[0]
    rows = start_basis.shape[2] // 2
    v = lax.axis_index("vec")
    n = lax.axis_size(AXES)
    groups = radix_groups(n)
    scale = 1.0 / (
        start_basis.shape[1] * start_basis.shape[2] * start_basis.shape[3] * lax.axis_size("space")
    )

    def in_order(a, b, axis):
        return jnp.where(v == 0, jnp.concatenate([a, b], axis), jnp.concatenate([b, a], axis))

    ext = jnp.concatenate([start_basis[:, :, -1:], start_basis, start_basis[:, :, :1]], axis=2)
    keep = lax.dynamic_slice_in_dim(ext, v * rows, rows + 2, 2)
    give = lax.dynamic_slice_in_dim(ext, (1 - v) * rows, rows + 2, 2)
    got = swap_vec(give)
    same_up = [(i, (i + 2) % n) for i in range(n)]
    same_down = [(j, i) for i, j in same_up]
    cross_up = [(i, ((i // 2 + 1) * 2 + 1 - i % 2) % n) for i in range(n)]
    cross_down = [(j, i) for i, j in cross_up]
    keep_rows = keep[:, :, 1:-1]
    give_rows = give[:, :, 1:-1]
    before = in_order(lax.ppermute(keep_rows, AXES, same_up), lax.ppermute(give_rows, AXES, cross_up), 0)
    after = in_order(lax.ppermute(keep_rows, AXES, same_down), lax.ppermute(give_rows, AXES, cross_down), 0)
    whole_ext = in_order(keep, got, 0)
    whole = whole_ext[:, :, 1:-1]
    ends = jnp.concatenate([whole_ext[:, :, :1], whole_ext[:, :, -1:]], axis=2)

    pot = lax.dynamic_slice_in_dim(potential, v * rows, rows, 1)
    shifted = jnp.where(pot >= SIGMA, pot - SIGMA + 6.0, pot - SIGMA - 6.0)

    h_whole = stencil(whole, (before, after, ends), pot)
    nb = whole.shape[0]
    fields = jnp.concatenate([whole, h_whole, whole / shifted, h_whole / shifted], 0)
    first = allsum(local_inner(fields[: 2 * nb], fields, scale), groups)
    gram = first[:nb, :nb]
    g_sh = first[:nb, nb:2 * nb]
    u_ss = first[:nb, 2 * nb:3 * nb]
    u_sh = first[:nb, 3 * nb:]
    u_hs = first[nb:, 2 * nb:3 * nb]
    u_hh = first[nb:, 3 * nb:]
    cmat = inverse_factor(gram).T
    ct = cmat.T
    rayleigh = mm(ct, mm(g_sh, cmat))
    b_b = mm(ct, mm(gram, cmat))
    ab_b = mm(ct, mm(g_sh.T, cmat)) - SIGMA * b_b

    cr = mm(cmat, rayleigh)
    s_rd = mm(u_sh, cmat) - mm(u_ss, cr)
    h_rd = mm(u_hh, cmat) - mm(u_hs, cr)
    coeff = -mm(ct, s_rd)
    ab_c = -mm(ct, h_rd - SIGMA * s_rd)
    back = ab_c - mm(ab_b, coeff)
    zero = jnp.zeros_like(cmat)
    weights = jnp.concatenate(
        [
            jnp.concatenate([cmat, -SIGMA * cmat, -cr, mm(cmat, coeff)], 1),
            jnp.concatenate([zero, cmat, cmat, zero], 1),
        ],
        0,
    )
    parts = combine(weights, jnp.concatenate([whole, h_whole], 0))
    both = parts[: 2 * nb]
    basis, a_basis, resid = parts[:nb], parts[nb:2 * nb], parts[2 * nb:3 * nb]
    correction = -resid / shifted
    proj = correction - parts[3 * nb:]
    pieces = halo(proj)

    moved = stencil(proj, pieces, pot) - SIGMA * proj
    correction = correction + (-resid - (moved - combine(back, basis))) / shifted

    for sweep in range(2, NSWEEP):
        pieces = halo(correction)
        red = allsum(local_inner(both, correction, scale), groups)
        coeff = red[:nb]
        back = red[nb:] - mm(ab_b, coeff)
        moved = stencil(correction, pieces, pot) - SIGMA * correction - combine(coeff, a_basis)
        correction = correction + (-resid - (moved - combine(back, basis))) / shifted

    red = allsum(
        jnp.concatenate([local_inner(basis, correction, scale), local_inner(correction, correction, scale)], 0),
        groups,
    )
    proj_two = red[:nb]
    gram_two = red[nb:] - 2.0 * mm(proj_two.T, proj_two) + mm(proj_two.T, mm(b_b, proj_two))
    fresh = correction - combine(proj_two, basis, PREC)
    new_all = combine(inverse_factor(gram_two).T, fresh, PREC)

    own = lax.dynamic_slice_in_dim(new_all, v * mine, mine, 0)
    out = lax.dynamic_slice_in_dim(new_all, (1 - v) * mine, mine, 0)
    new_basis = in_order(own, swap_vec(out), 2)
    return (new_basis, rayleigh)


def solution(mesh):
    in_specs = (P("space", None, None), P("vec", "space", None, None))
    out_specs = (P("vec", "space", None, None), P())
    return jax.shard_map(local, mesh=mesh, in_specs=in_specs, out_specs=out_specs, check_vma=False)
```

```python
import jax
import jax.numpy as jnp
from jax import lax
from jax.sharding import PartitionSpec as P

NSWEEP = 3


SIGMA = 0.5
PREC = lax.Precision.HIGHEST
FIELD_PREC = lax.Precision.HIGH
AXES = ("space", "vec")


def allsum(x, groups):
    n = lax.axis_size(AXES)
    for group in groups:
        vals = {0: x}
        for m in range(1, 1 << len(group)):
            mask = sum(1 << b for t, b in enumerate(group) if (m >> t) & 1)
            vals[m] = lax.ppermute(x, AXES, [(i, i ^ mask) for i in range(n)])
        for t in range(len(group)):
            vals = {m: vals[m] + vals[m | (1 << t)] for m in vals if not (m >> t) & 1}
        x = vals[0]
    return x


def radix_groups(n):
    bits = n.bit_length() - 1
    return [[0]] + [list(range(i, min(i + 2, bits))) for i in range(1, bits, 2)]


def local_inner(left, right, scale):
    return jnp.einsum("kzyx,jzyx->kj", left, right, precision=FIELD_PREC) * scale


def combine(coeff, vectors, precision=FIELD_PREC):
    return jnp.einsum("kj,kzyx->jzyx", coeff, vectors, precision=precision)


def mm(a, b):
    return jnp.matmul(a, b, precision=PREC)


def swap_vec(value):
    return lax.ppermute(value, "vec", [(0, 1), (1, 0)])


def halo(value):
    peers = lax.axis_size("space")
    up = [(i, (i + 1) % peers) for i in range(peers)]
    down = [(j, i) for i, j in up]
    rows = value.shape[2]
    edge = jnp.concatenate([value[:, :, rows - 1:], value[:, :, :1]], axis=2)
    before = lax.ppermute(value, "space", up)
    after = lax.ppermute(value, "space", down)
    ends = swap_vec(edge)
    return before, after, ends


def stencil(value, pieces, potential):
    before, after, ends = pieces
    ext = jnp.concatenate([ends[:, :, :1], value, ends[:, :, 1:]], axis=2)
    beside = before + after
    beside = beside + ext[:, :, :-2] + ext[:, :, 2:]
    beside = beside + jnp.roll(value, 1, 3) + jnp.roll(value, -1, 3)
    return potential * value - beside


def inverse_factor(gram):
    lower = jnp.linalg.cholesky(gram)
    return jax.scipy.linalg.solve_triangular(
        lower, jnp.eye(gram.shape[0], dtype=jnp.float32), lower=True
    )


def local(potential, start_basis):
    mine = start_basis.shape[0]
    rows = start_basis.shape[2] // 2
    v = lax.axis_index("vec")
    n = lax.axis_size(AXES)
    groups = radix_groups(n)
    scale = 1.0 / (
        start_basis.shape[1] * start_basis.shape[2] * start_basis.shape[3] * lax.axis_size("space")
    )

    def in_order(a, b, axis):
        return jnp.where(v == 0, jnp.concatenate([a, b], axis), jnp.concatenate([b, a], axis))

    ext = jnp.concatenate([start_basis[:, :, -1:], start_basis, start_basis[:, :, :1]], axis=2)
    keep = lax.dynamic_slice_in_dim(ext, v * rows, rows + 2, 2)
    give = lax.dynamic_slice_in_dim(ext, (1 - v) * rows, rows + 2, 2)
    got = swap_vec(give)
    same_up = [(i, (i + 2) % n) for i in range(n)]
    same_down = [(j, i) for i, j in same_up]
    cross_up = [(i, ((i // 2 + 1) * 2 + 1 - i % 2) % n) for i in range(n)]
    cross_down = [(j, i) for i, j in cross_up]
    keep_rows = keep[:, :, 1:-1]
    give_rows = give[:, :, 1:-1]
    before = in_order(lax.ppermute(keep_rows, AXES, same_up), lax.ppermute(give_rows, AXES, cross_up), 0)
    after = in_order(lax.ppermute(keep_rows, AXES, same_down), lax.ppermute(give_rows, AXES, cross_down), 0)
    whole_ext = in_order(keep, got, 0)
    whole = whole_ext[:, :, 1:-1]
    ends = jnp.concatenate([whole_ext[:, :, :1], whole_ext[:, :, -1:]], axis=2)

    pot = lax.dynamic_slice_in_dim(potential, v * rows, rows, 1)
    shifted = jnp.where(pot >= SIGMA, pot - SIGMA + 6.0, pot - SIGMA - 6.0)

    h_whole = stencil(whole, (before, after, ends), pot)
    nb = whole.shape[0]
    fields = jnp.concatenate([whole, h_whole], 0)
    first = allsum(
        jnp.concatenate(
            [local_inner(fields, fields, scale), local_inner(fields, fields / shifted, scale)], 1
        ),
        groups,
    )
    gram = first[:nb, :nb]
    g_sh = first[:nb, nb:2 * nb]
    u_ss = first[:nb, 2 * nb:3 * nb]
    u_sh = first[:nb, 3 * nb:]
    u_hs = first[nb:, 2 * nb:3 * nb]
    u_hh = first[nb:, 3 * nb:]
    cmat = inverse_factor(gram).T
    ct = cmat.T
    rayleigh = mm(ct, mm(g_sh, cmat))
    b_b = mm(ct, mm(gram, cmat))
    ab_b = mm(ct, mm(g_sh.T, cmat)) - SIGMA * b_b

    cr = mm(cmat, rayleigh)
    s_rd = mm(u_sh, cmat) - mm(u_ss, cr)
    h_rd = mm(u_hh, cmat) - mm(u_hs, cr)
    coeff = -mm(ct, s_rd)
    ab_c = -mm(ct, h_rd - SIGMA * s_rd)
    back = ab_c - mm(ab_b, coeff)
    zero = jnp.zeros_like(cmat)
    weights = jnp.concatenate(
        [
            jnp.concatenate([cmat, -SIGMA * cmat, -cr, mm(cmat, coeff)], 1),
            jnp.concatenate([zero, cmat, cmat, zero], 1),
        ],
        0,
    )
    parts = combine(weights, jnp.concatenate([whole, h_whole], 0))
    both = parts[: 2 * nb]
    basis, a_basis, resid = parts[:nb], parts[nb:2 * nb], parts[2 * nb:3 * nb]
    correction = -resid / shifted
    proj = correction - parts[3 * nb:]
    pieces = halo(proj)

    moved = stencil(proj, pieces, pot) - SIGMA * proj
    correction = correction + (-resid - (moved - combine(back, basis))) / shifted

    for sweep in range(2, NSWEEP):
        pieces = halo(correction)
        red = allsum(local_inner(both, correction, scale), groups)
        coeff = red[:nb]
        back = red[nb:] - mm(ab_b, coeff)
        moved = stencil(correction, pieces, pot) - SIGMA * correction - combine(coeff, a_basis)
        correction = correction + (-resid - (moved - combine(back, basis))) / shifted

    red = allsum(
        jnp.concatenate([local_inner(basis, correction, scale), local_inner(correction, correction, scale)], 0),
        groups,
    )
    proj_two = red[:nb]
    gram_two = red[nb:] - 2.0 * mm(proj_two.T, proj_two) + mm(proj_two.T, mm(b_b, proj_two))
    fresh = correction - combine(proj_two, basis, PREC)
    new_all = combine(inverse_factor(gram_two).T, fresh, PREC)

    own = lax.dynamic_slice_in_dim(new_all, v * mine, mine, 0)
    out = lax.dynamic_slice_in_dim(new_all, (1 - v) * mine, mine, 0)
    new_basis = in_order(own, swap_vec(out), 2)
    return (new_basis, rayleigh)


def solution(mesh):
    in_specs = (P("space", None, None), P("vec", "space", None, None))
    out_specs = (P("vec", "space", None, None), P())
    return jax.shard_map(local, mesh=mesh, in_specs=in_specs, out_specs=out_specs, check_vma=False)
```

```python
import jax
import jax.numpy as jnp
from jax import lax
from jax.sharding import PartitionSpec as P

NSWEEP = 3


SIGMA = 0.5
PREC = lax.Precision.HIGHEST
FIELD_PREC = lax.Precision.HIGH
AXES = ("space", "vec")


def allsum(x, groups):
    n = lax.axis_size(AXES)
    for group in groups:
        vals = {0: x}
        for m in range(1, 1 << len(group)):
            mask = sum(1 << b for t, b in enumerate(group) if (m >> t) & 1)
            vals[m] = lax.ppermute(x, AXES, [(i, i ^ mask) for i in range(n)])
        for t in range(len(group)):
            vals = {m: vals[m] + vals[m | (1 << t)] for m in vals if not (m >> t) & 1}
        x = vals[0]
    return x


def radix_groups(n):
    bits = n.bit_length() - 1
    return [[0]] + [list(range(i, min(i + 2, bits))) for i in range(1, bits, 2)]


def local_inner(left, right, scale):
    return jnp.einsum("kzyx,jzyx->kj", left, right, precision=FIELD_PREC) * scale


def combine(coeff, vectors, precision=FIELD_PREC):
    return jnp.einsum("kj,kzyx->jzyx", coeff, vectors, precision=precision)


def mm(a, b):
    return jnp.matmul(a, b, precision=PREC)


def swap_vec(value):
    return lax.ppermute(value, "vec", [(0, 1), (1, 0)])


def halo(value):
    peers = lax.axis_size("space")
    up = [(i, (i + 1) % peers) for i in range(peers)]
    down = [(j, i) for i, j in up]
    rows = value.shape[2]
    edge = jnp.concatenate([value[:, :, rows - 1:], value[:, :, :1]], axis=2)
    before = lax.ppermute(value, "space", up)
    after = lax.ppermute(value, "space", down)
    ends = swap_vec(edge)
    return before, after, ends


def stencil(value, pieces, potential):
    before, after, ends = pieces
    ext = jnp.concatenate([ends[:, :, :1], value, ends[:, :, 1:]], axis=2)
    beside = before + after
    beside = beside + ext[:, :, :-2] + ext[:, :, 2:]
    beside = beside + jnp.roll(value, 1, 3) + jnp.roll(value, -1, 3)
    return potential * value - beside


def inverse_factor(gram):
    lower = jnp.linalg.cholesky(gram)
    return jax.scipy.linalg.solve_triangular(
        lower, jnp.eye(gram.shape[0], dtype=jnp.float32), lower=True
    )


def local(potential, start_basis):
    mine = start_basis.shape[0]
    rows = start_basis.shape[2] // 2
    v = lax.axis_index("vec")
    n = lax.axis_size(AXES)
    groups = radix_groups(n)
    scale = 1.0 / (
        start_basis.shape[1] * start_basis.shape[2] * start_basis.shape[3] * lax.axis_size("space")
    )

    def in_order(a, b, axis):
        return jnp.where(v == 0, jnp.concatenate([a, b], axis), jnp.concatenate([b, a], axis))

    ext = jnp.concatenate([start_basis[:, :, -1:], start_basis, start_basis[:, :, :1]], axis=2)
    keep = lax.dynamic_slice_in_dim(ext, v * rows, rows + 2, 2)
    give = lax.dynamic_slice_in_dim(ext, (1 - v) * rows, rows + 2, 2)
    got = swap_vec(give)
    same_up = [(i, (i + 2) % n) for i in range(n)]
    same_down = [(j, i) for i, j in same_up]
    cross_up = [(i, ((i // 2 + 1) * 2 + 1 - i % 2) % n) for i in range(n)]
    cross_down = [(j, i) for i, j in cross_up]
    keep_rows = keep[:, :, 1:-1]
    give_rows = give[:, :, 1:-1]
    before = in_order(lax.ppermute(keep_rows, AXES, same_up), lax.ppermute(give_rows, AXES, cross_up), 0)
    after = in_order(lax.ppermute(keep_rows, AXES, same_down), lax.ppermute(give_rows, AXES, cross_down), 0)
    whole_ext = in_order(keep, got, 0)
    whole = whole_ext[:, :, 1:-1]
    ends = jnp.concatenate([whole_ext[:, :, :1], whole_ext[:, :, -1:]], axis=2)

    pot = lax.dynamic_slice_in_dim(potential, v * rows, rows, 1)
    shifted = jnp.where(pot >= SIGMA, pot - SIGMA + 6.0, pot - SIGMA - 6.0)

    h_whole = stencil(whole, (before, after, ends), pot)
    nb = whole.shape[0]
    fields = jnp.concatenate([whole, h_whole, whole / shifted, h_whole / shifted], 0)
    first = allsum(local_inner(fields[: 2 * nb], fields, scale), groups)
    gram = first[:nb, :nb]
    g_sh = first[:nb, nb:2 * nb]
    u_ss = first[:nb, 2 * nb:3 * nb]
    u_sh = first[:nb, 3 * nb:]
    u_hs = first[nb:, 2 * nb:3 * nb]
    u_hh = first[nb:, 3 * nb:]
    cmat = inverse_factor(gram).T
    ct = cmat.T
    rayleigh = mm(ct, mm(g_sh, cmat))
    b_b = mm(ct, mm(gram, cmat))
    ab_b = mm(ct, mm(g_sh.T, cmat)) - SIGMA * b_b

    cr = mm(cmat, rayleigh)
    s_rd = mm(u_sh, cmat) - mm(u_ss, cr)
    h_rd = mm(u_hh, cmat) - mm(u_hs, cr)
    coeff = -mm(ct, s_rd)
    ab_c = -mm(ct, h_rd - SIGMA * s_rd)
    back = ab_c - mm(ab_b, coeff)
    zero = jnp.zeros_like(cmat)
    weights = jnp.concatenate(
        [
            jnp.concatenate([cmat, -SIGMA * cmat, -cr, mm(cmat, coeff)], 1),
            jnp.concatenate([zero, cmat, cmat, zero], 1),
        ],
        0,
    )
    parts = combine(weights, jnp.concatenate([whole, h_whole], 0))
    both = parts[: 2 * nb]
    basis, a_basis, resid = parts[:nb], parts[nb:2 * nb], parts[2 * nb:3 * nb]
    correction = -resid / shifted
    proj = correction - parts[3 * nb:]
    pieces = halo(proj)

    moved = stencil(proj, pieces, pot) - SIGMA * proj
    correction = correction + (-resid - (moved - combine(back, basis))) / shifted

    for sweep in range(2, NSWEEP):
        pieces = halo(correction)
        red = allsum(local_inner(both, correction, scale), groups)
        coeff = red[:nb]
        back = red[nb:] - mm(ab_b, coeff)
        moved = stencil(correction, pieces, pot) - SIGMA * correction - combine(coeff, a_basis)
        correction = correction + (-resid - (moved - combine(back, basis))) / shifted

    red = allsum(
        jnp.concatenate([local_inner(basis, correction, scale), local_inner(correction, correction, scale)], 0),
        groups,
    )
    proj_two = red[:nb]
    gram_two = red[nb:] - 2.0 * mm(proj_two.T, proj_two) + mm(proj_two.T, mm(b_b, proj_two))
    c_two = inverse_factor(gram_two).T
    new_all = combine(
        jnp.concatenate([c_two, -mm(proj_two, c_two)], 0), jnp.concatenate([correction, basis], 0), PREC
    )

    own = lax.dynamic_slice_in_dim(new_all, v * mine, mine, 0)
    out = lax.dynamic_slice_in_dim(new_all, (1 - v) * mine, mine, 0)
    new_basis = in_order(own, swap_vec(out), 2)
    return (new_basis, rayleigh)


def solution(mesh):
    in_specs = (P("space", None, None), P("vec", "space", None, None))
    out_specs = (P("vec", "space", None, None), P())
    return jax.shard_map(local, mesh=mesh, in_specs=in_specs, out_specs=out_specs, check_vma=False)
```

```python
import jax
import jax.numpy as jnp
from jax import lax
from jax.sharding import PartitionSpec as P

NSWEEP = 3


SIGMA = 0.5
PREC = lax.Precision.HIGHEST
FIELD_PREC = lax.Precision.HIGH
AXES = ("space", "vec")


def allsum(x, groups):
    n = lax.axis_size(AXES)
    for group in groups:
        vals = {0: x}
        for m in range(1, 1 << len(group)):
            mask = sum(1 << b for t, b in enumerate(group) if (m >> t) & 1)
            vals[m] = lax.ppermute(x, AXES, [(i, i ^ mask) for i in range(n)])
        for t in range(len(group)):
            vals = {m: vals[m] + vals[m | (1 << t)] for m in vals if not (m >> t) & 1}
        x = vals[0]
    return x


def radix_groups(n):
    bits = n.bit_length() - 1
    return [[0]] + [list(range(i, min(i + 2, bits))) for i in range(1, bits, 2)]


def local_inner(left, right, scale):
    return jnp.einsum("kzyx,jzyx->kj", left, right, precision=FIELD_PREC) * scale


def combine(coeff, vectors, precision=FIELD_PREC):
    return jnp.einsum("kj,kzyx->jzyx", coeff, vectors, precision=precision)


def mm(a, b):
    return jnp.matmul(a, b, precision=PREC)


def swap_vec(value):
    return lax.ppermute(value, "vec", [(0, 1), (1, 0)])


def halo(value):
    peers = lax.axis_size("space")
    up = [(i, (i + 1) % peers) for i in range(peers)]
    down = [(j, i) for i, j in up]
    rows = value.shape[2]
    edge = jnp.concatenate([value[:, :, rows - 1:], value[:, :, :1]], axis=2)
    before = lax.ppermute(value, "space", up)
    after = lax.ppermute(value, "space", down)
    ends = swap_vec(edge)
    return before, after, ends


def stencil(value, pieces, potential):
    before, after, ends = pieces
    ext = jnp.concatenate([ends[:, :, :1], value, ends[:, :, 1:]], axis=2)
    beside = before + after
    beside = beside + ext[:, :, :-2] + ext[:, :, 2:]
    beside = beside + jnp.roll(value, 1, 3) + jnp.roll(value, -1, 3)
    return potential * value - beside


def inverse_factor(gram):
    lower = jnp.linalg.cholesky(gram)
    return jax.scipy.linalg.solve_triangular(
        lower, jnp.eye(gram.shape[0], dtype=jnp.float32), lower=True
    )


def local(potential, start_basis):
    mine = start_basis.shape[0]
    rows = start_basis.shape[2] // 2
    v = lax.axis_index("vec")
    n = lax.axis_size(AXES)
    groups = radix_groups(n)
    scale = 1.0 / (
        start_basis.shape[1] * start_basis.shape[2] * start_basis.shape[3] * lax.axis_size("space")
    )

    def in_order(a, b, axis):
        return jnp.where(v == 0, jnp.concatenate([a, b], axis), jnp.concatenate([b, a], axis))

    ext = jnp.concatenate([start_basis[:, :, -1:], start_basis, start_basis[:, :, :1]], axis=2)
    keep = lax.dynamic_slice_in_dim(ext, v * rows, rows + 2, 2)
    give = lax.dynamic_slice_in_dim(ext, (1 - v) * rows, rows + 2, 2)
    got = swap_vec(give)
    same_up = [(i, (i + 2) % n) for i in range(n)]
    same_down = [(j, i) for i, j in same_up]
    cross_up = [(i, ((i // 2 + 1) * 2 + 1 - i % 2) % n) for i in range(n)]
    cross_down = [(j, i) for i, j in cross_up]
    keep_rows = keep[:, :, 1:-1]
    give_rows = give[:, :, 1:-1]
    before = in_order(lax.ppermute(keep_rows, AXES, same_up), lax.ppermute(give_rows, AXES, cross_up), 0)
    after = in_order(lax.ppermute(keep_rows, AXES, same_down), lax.ppermute(give_rows, AXES, cross_down), 0)
    whole_ext = in_order(keep, got, 0)
    whole = whole_ext[:, :, 1:-1]
    ends = jnp.concatenate([whole_ext[:, :, :1], whole_ext[:, :, -1:]], axis=2)

    pot = lax.dynamic_slice_in_dim(potential, v * rows, rows, 1)
    shifted = jnp.where(pot >= SIGMA, pot - SIGMA + 6.0, pot - SIGMA - 6.0)

    h_whole = stencil(whole, (before, after, ends), pot)
    nb = whole.shape[0]
    fields = jnp.concatenate([whole, h_whole, whole / shifted, h_whole / shifted], 0)
    first = allsum(local_inner(fields[: 2 * nb], fields, scale), groups)
    gram = first[:nb, :nb]
    g_sh = first[:nb, nb:2 * nb]
    u_ss = first[:nb, 2 * nb:3 * nb]
    u_sh = first[:nb, 3 * nb:]
    u_hs = first[nb:, 2 * nb:3 * nb]
    u_hh = first[nb:, 3 * nb:]
    cmat = inverse_factor(gram).T
    ct = cmat.T
    rayleigh = mm(ct, mm(g_sh, cmat))
    b_b = mm(ct, mm(gram, cmat))
    ab_b = mm(ct, mm(g_sh.T, cmat)) - SIGMA * b_b

    cr = mm(cmat, rayleigh)
    s_rd = mm(u_sh, cmat) - mm(u_ss, cr)
    h_rd = mm(u_hh, cmat) - mm(u_hs, cr)
    coeff = -mm(ct, s_rd)
    ab_c = -mm(ct, h_rd - SIGMA * s_rd)
    back = ab_c - mm(ab_b, coeff)
    zero = jnp.zeros_like(cmat)
    weights = jnp.concatenate(
        [
            jnp.concatenate([cmat, -SIGMA * cmat, -cr, mm(cmat, coeff)], 1),
            jnp.concatenate([zero, cmat, cmat, zero], 1),
        ],
        0,
    )
    parts = combine(weights, jnp.concatenate([whole, h_whole], 0))
    both = parts[: 2 * nb]
    basis, a_basis, resid = parts[:nb], parts[nb:2 * nb], parts[2 * nb:3 * nb]
    correction = -resid / shifted
    proj = correction - parts[3 * nb:]
    pieces = halo(proj)

    moved = stencil(proj, pieces, pot) - SIGMA * proj
    correction = correction + (-resid - (moved - combine(back, basis))) / shifted

    for sweep in range(2, NSWEEP):
        pieces = halo(correction)
        red = allsum(local_inner(both, correction, scale), groups)
        coeff = red[:nb]
        back = red[nb:] - mm(ab_b, coeff)
        mixed = combine(jnp.concatenate([back, coeff], 0), both)
        moved = stencil(correction, pieces, pot) - SIGMA * correction
        correction = correction + (-resid - (moved - mixed)) / shifted

    red = allsum(
        jnp.concatenate([local_inner(basis, correction, scale), local_inner(correction, correction, scale)], 0),
        groups,
    )
    proj_two = red[:nb]
    gram_two = red[nb:] - 2.0 * mm(proj_two.T, proj_two) + mm(proj_two.T, mm(b_b, proj_two))
    c_two = inverse_factor(gram_two).T
    new_all = combine(
        jnp.concatenate([c_two, -mm(proj_two, c_two)], 0), jnp.concatenate([correction, basis], 0), PREC
    )

    own = lax.dynamic_slice_in_dim(new_all, v * mine, mine, 0)
    out = lax.dynamic_slice_in_dim(new_all, (1 - v) * mine, mine, 0)
    new_basis = in_order(own, swap_vec(out), 2)
    return (new_basis, rayleigh)


def solution(mesh):
    in_specs = (P("space", None, None), P("vec", "space", None, None))
    out_specs = (P("vec", "space", None, None), P())
    return jax.shard_map(local, mesh=mesh, in_specs=in_specs, out_specs=out_specs, check_vma=False)
```

```python
import jax
import jax.numpy as jnp
from jax import lax
from jax.sharding import PartitionSpec as P

NSWEEP = 3


SIGMA = 0.5
PREC = lax.Precision.HIGHEST
FIELD_PREC = lax.Precision.HIGH
AXES = ("space", "vec")


def allsum(x, groups):
    n = lax.axis_size(AXES)
    for group in groups:
        vals = {0: x}
        for m in range(1, 1 << len(group)):
            mask = sum(1 << b for t, b in enumerate(group) if (m >> t) & 1)
            vals[m] = lax.ppermute(x, AXES, [(i, i ^ mask) for i in range(n)])
        for t in range(len(group)):
            vals = {m: vals[m] + vals[m | (1 << t)] for m in vals if not (m >> t) & 1}
        x = vals[0]
    return x


def radix_groups(n):
    bits = n.bit_length() - 1
    return [[0]] + [list(range(i, min(i + 2, bits))) for i in range(1, bits, 2)]


def local_inner(left, right, scale):
    return jnp.einsum("kzyx,jzyx->kj", left, right, precision=FIELD_PREC) * scale


def combine(coeff, vectors, precision=FIELD_PREC):
    return jnp.einsum("kj,kzyx->jzyx", coeff, vectors, precision=precision)


def mm(a, b):
    return jnp.matmul(a, b, precision=PREC)


def swap_vec(value):
    return lax.ppermute(value, "vec", [(0, 1), (1, 0)])


def halo(value):
    peers = lax.axis_size("space")
    up = [(i, (i + 1) % peers) for i in range(peers)]
    down = [(j, i) for i, j in up]
    rows = value.shape[2]
    edge = jnp.concatenate([value[:, :, rows - 1:], value[:, :, :1]], axis=2)
    before = lax.ppermute(value, "space", up)
    after = lax.ppermute(value, "space", down)
    ends = swap_vec(edge)
    return before, after, ends


def stencil(value, pieces, potential):
    before, after, ends = pieces
    ext = jnp.concatenate([ends[:, :, :1], value, ends[:, :, 1:]], axis=2)
    beside = before + after
    beside = beside + ext[:, :, :-2] + ext[:, :, 2:]
    beside = beside + jnp.roll(value, 1, 3) + jnp.roll(value, -1, 3)
    return potential * value - beside


def inverse_factor(gram):
    lower = jnp.linalg.cholesky(gram)
    return jax.scipy.linalg.solve_triangular(
        lower, jnp.eye(gram.shape[0], dtype=jnp.float32), lower=True
    )


def local(potential, start_basis):
    mine = start_basis.shape[0]
    rows = start_basis.shape[2] // 2
    v = lax.axis_index("vec")
    n = lax.axis_size(AXES)
    groups = radix_groups(n)
    scale = 1.0 / (
        start_basis.shape[1] * start_basis.shape[2] * start_basis.shape[3] * lax.axis_size("space")
    )

    def in_order(a, b, axis):
        return jnp.where(v == 0, jnp.concatenate([a, b], axis), jnp.concatenate([b, a], axis))

    ext = jnp.concatenate([start_basis[:, :, -1:], start_basis, start_basis[:, :, :1]], axis=2)
    keep = lax.dynamic_slice_in_dim(ext, v * rows, rows + 2, 2)
    give = lax.dynamic_slice_in_dim(ext, (1 - v) * rows, rows + 2, 2)
    got = swap_vec(give)
    same_up = [(i, (i + 2) % n) for i in range(n)]
    same_down = [(j, i) for i, j in same_up]
    cross_up = [(i, ((i // 2 + 1) * 2 + 1 - i % 2) % n) for i in range(n)]
    cross_down = [(j, i) for i, j in cross_up]
    keep_rows = keep[:, :, 1:-1]
    give_rows = give[:, :, 1:-1]
    before = in_order(lax.ppermute(keep_rows, AXES, same_up), lax.ppermute(give_rows, AXES, cross_up), 0)
    after = in_order(lax.ppermute(keep_rows, AXES, same_down), lax.ppermute(give_rows, AXES, cross_down), 0)
    whole_ext = in_order(keep, got, 0)
    whole = whole_ext[:, :, 1:-1]
    ends = jnp.concatenate([whole_ext[:, :, :1], whole_ext[:, :, -1:]], axis=2)

    pot = lax.dynamic_slice_in_dim(potential, v * rows, rows, 1)
    shifted = jnp.where(pot >= SIGMA, pot - SIGMA + 6.0, pot - SIGMA - 6.0)

    h_whole = stencil(whole, (before, after, ends), pot)
    nb = whole.shape[0]
    fields = jnp.concatenate([whole, h_whole, whole / shifted, h_whole / shifted], 0)
    first = allsum(local_inner(fields[: 2 * nb], fields, scale), groups)
    gram = first[:nb, :nb]
    g_sh = first[:nb, nb:2 * nb]
    u_ss = first[:nb, 2 * nb:3 * nb]
    u_sh = first[:nb, 3 * nb:]
    u_hs = first[nb:, 2 * nb:3 * nb]
    u_hh = first[nb:, 3 * nb:]
    cmat = inverse_factor(gram).T
    ct = cmat.T
    rayleigh = mm(ct, mm(g_sh, cmat))
    b_b = mm(ct, mm(gram, cmat))
    ab_b = mm(ct, mm(g_sh.T, cmat)) - SIGMA * b_b

    cr = mm(cmat, rayleigh)
    s_rd = mm(u_sh, cmat) - mm(u_ss, cr)
    h_rd = mm(u_hh, cmat) - mm(u_hs, cr)
    coeff = -mm(ct, s_rd)
    ab_c = -mm(ct, h_rd - SIGMA * s_rd)
    back = ab_c - mm(ab_b, coeff)
    zero = jnp.zeros_like(cmat)
    weights = jnp.concatenate(
        [
            jnp.concatenate([cmat, -SIGMA * cmat, -cr, mm(cmat, coeff), mm(cmat, back)], 1),
            jnp.concatenate([zero, cmat, cmat, zero, zero], 1),
        ],
        0,
    )
    parts = combine(weights, jnp.concatenate([whole, h_whole], 0))
    both = parts[: 2 * nb]
    basis, a_basis, resid = parts[:nb], parts[nb:2 * nb], parts[2 * nb:3 * nb]
    correction = -resid / shifted
    proj = correction - parts[3 * nb:4 * nb]
    pieces = halo(proj)

    moved = stencil(proj, pieces, pot) - SIGMA * proj
    correction = correction + (-resid - (moved - parts[4 * nb:])) / shifted

    for sweep in range(2, NSWEEP):
        pieces = halo(correction)
        red = allsum(local_inner(both, correction, scale), groups)
        coeff = red[:nb]
        back = red[nb:] - mm(ab_b, coeff)
        mixed = combine(jnp.concatenate([back, coeff], 0), both)
        moved = stencil(correction, pieces, pot) - SIGMA * correction
        correction = correction + (-resid - (moved - mixed)) / shifted

    red = allsum(
        jnp.concatenate([local_inner(basis, correction, scale), local_inner(correction, correction, scale)], 0),
        groups,
    )
    proj_two = red[:nb]
    gram_two = red[nb:] - 2.0 * mm(proj_two.T, proj_two) + mm(proj_two.T, mm(b_b, proj_two))
    c_two = inverse_factor(gram_two).T
    new_all = combine(
        jnp.concatenate([c_two, -mm(proj_two, c_two)], 0), jnp.concatenate([correction, basis], 0), PREC
    )

    own = lax.dynamic_slice_in_dim(new_all, v * mine, mine, 0)
    out = lax.dynamic_slice_in_dim(new_all, (1 - v) * mine, mine, 0)
    new_basis = in_order(own, swap_vec(out), 2)
    return (new_basis, rayleigh)


def solution(mesh):
    in_specs = (P("space", None, None), P("vec", "space", None, None))
    out_specs = (P("vec", "space", None, None), P())
    return jax.shard_map(local, mesh=mesh, in_specs=in_specs, out_specs=out_specs, check_vma=False)
```
